32 devices in a mesh: dp: 2 (over x), mp: 16 (over z, y, core).
Axes of the slice: x: 2, y: 2, z: 4, core: 2. Of those that a mesh axis runs over, the one named last changes fastest.
Arguments:
- inputs: bfloat16 [256, 8192], P('dp', 'mp'), may hold values from -6 to 6
- out_grad: bfloat16 [256, 8192], P('dp', 'mp'), may hold values from -6 to 6
- w_in: bfloat16 [128, 4, 128, 128], P('mp'), may hold values from -0.25 to 0.25
- in_blocks: int32 [128, 4], P('mp'), may hold values from 0 to 63, as said below
- w_out: bfloat16 [128, 4, 128, 128], P('mp'), may hold values from -0.1875 to 0.1875
- out_blocks: int32 [128, 4], P('mp'), may hold values from 0 to 63, as said below
Outputs:
- outputs: bfloat16 [256, 8192], P('dp', 'mp')
- in_grad: bfloat16 [256, 8192], P('dp', 'mp')
- w_in_grad: bfloat16 [128, 4, 128, 128], P('mp')
- w_out_grad: bfloat16 [128, 4, 128, 128], P('mp')
The draws below stay inside these ranges and needn't reach their ends.
Inputs may be any that keep to these rules, and one draw needn't show every extreme that they name: `in_blocks`: the 4 input column blocks of one hidden block row are distinct. `out_blocks`: the 4 output column blocks of one hidden block row are distinct.
All inputs are finite; a program needn't handle non-finite values.
Results may differ from the reference program's by a relative error of at most 0.017.
Values may be sent and summed in bfloat16 or wider, within the bound.
No kernel may reach another device: no remote copies, remote signals or barrier semaphores. Data moves between devices by JAX's collectives and lax.ppermute only.
A program may use at most 64 MiB of HBM per device.

```python
import jax
import jax.numpy as jnp
from jax import lax

D = 8192
BLK = 128
HB_DEV = 8
TOK = 128
KB = 4
HBLK = 128
H = 16384
TOKENS = 256
N_DP = 2
N_MP = 16


def block_pattern(key, row_count, col_count, take_count):
    scores = jax.random.randint(key, (row_count, col_count), 0, 1 << 20)
    scores = scores * col_count + jnp.arange(col_count, dtype=jnp.int32)[None, :]
    order = jnp.argsort(scores, axis=1, stable=True)
    return order[:, :take_count].astype(jnp.int32)


def draw_in_blocks(key, part):
    return block_pattern(jax.random.fold_in(key, 11), HBLK, D // BLK, KB)


def draw_out_blocks(key, part):
    return block_pattern(jax.random.fold_in(key, 23), HBLK, D // BLK, KB)


def block_scale(key, extent, cuts, smallest, largest):
    def one(axis_at, parts):
        steps = jax.random.uniform(jax.random.fold_in(jax.random.fold_in(key, 6), axis_at), (parts,), jnp.float32, smallest / len(cuts), largest / len(cuts))
        return jnp.repeat(jnp.exp(steps), extent[axis_at] // parts).reshape((-1,) + (1,) * (len(extent) - axis_at - 1))

    factor_of = one(*cuts[0])
    for cut in cuts[1:]:
        factor_of = factor_of * one(*cut)
    return factor_of


def noise(own_key, extent, spread, reach, split=(), held_as=jnp.bfloat16):
    drawn = spread * jax.random.normal(own_key, extent, jnp.float32)
    if split:
        drawn = drawn * block_scale(own_key, extent, split, -0.22, 0.18)
    return jnp.clip(drawn, -reach, reach).astype(held_as)


def setup_inputs(seed: int = 0) -> dict:
    keys = jax.random.split(jax.random.key(seed), 7)
    inputs = noise(keys[0], (TOKENS, D), 1.0, 6.0, ((0, 2), (1, 16)))
    out_grad = noise(keys[1], (TOKENS, D), 1.0, 6.0, ((0, 2), (1, 16)))
    w_in = noise(keys[2], (HBLK, KB, BLK, BLK), (KB * BLK) ** -0.5, 0.25, ((0, 16),))
    in_blocks = draw_in_blocks(jax.random.fold_in(keys[6], 71), 0)
    w_out = noise(keys[4], (HBLK, KB, BLK, BLK), (H * KB * BLK // D) ** -0.5, 0.1875, ((0, 16),))
    out_blocks = draw_out_blocks(jax.random.fold_in(keys[6], 71), 0)
    return dict(inputs=inputs, out_grad=out_grad, w_in=w_in, in_blocks=in_blocks, w_out=w_out, out_blocks=out_blocks)


root_half = 0.7071067811865476
inv_root_two_pi = 0.3989422804014327


def gelu_value(preact):
    return 0.5 * preact * (1.0 + jax.scipy.special.erf(preact * root_half))


def gelu_slope(preact):
    return 0.5 * (1.0 + jax.scipy.special.erf(preact * root_half)) + preact * jnp.exp(-0.5 * preact * preact) * inv_root_two_pi


def round_half(values):
    rounded = lax.optimization_barrier(values.astype(jnp.bfloat16))
    return rounded.astype(jnp.float32)


def reference(inputs, out_grad, w_in, in_blocks, w_out, out_blocks):
    tok_total = inputs.shape[0]
    col_count = D // BLK
    pair_count = HB_DEV * KB
    in_view = inputs.reshape(tok_total, col_count, BLK).astype(jnp.float32)
    grad_view = out_grad.reshape(tok_total, col_count, BLK).astype(jnp.float32)
    columns = jnp.arange(col_count, dtype=jnp.int32)
    w_in_group = w_in.reshape(N_MP, HB_DEV, KB, BLK, BLK)
    w_out_group = w_out.reshape(N_MP, HB_DEV, KB, BLK, BLK)
    in_group = in_blocks.reshape(N_MP, HB_DEV, KB).astype(jnp.int32)
    out_group = out_blocks.reshape(N_MP, HB_DEV, KB).astype(jnp.int32)

    def scan_step(totals, slab_data):
        out_total, in_total = totals
        w_in_slab, in_slab, w_out_slab, out_slab = slab_data
        w_in_wide = w_in_slab.astype(jnp.float32)
        w_out_wide = w_out_slab.astype(jnp.float32)
        in_flat = in_slab.reshape(pair_count)
        out_flat = out_slab.reshape(pair_count)
        in_sel = jnp.take(in_view, in_flat, axis=1).reshape(tok_total, HB_DEV, KB, BLK)
        grad_sel = jnp.take(grad_view, out_flat, axis=1).reshape(tok_total, HB_DEV, KB, BLK)
        preact = jnp.einsum("trki,rkio->tro", in_sel, w_in_wide)
        hidden = round_half(gelu_value(preact))
        out_terms = jnp.einsum("tri,rkio->trko", hidden, w_out_wide).reshape(tok_total, pair_count, BLK)
        out_onehot = (out_flat[:, None] == columns[None, :]).astype(jnp.float32)
        out_total = out_total + jnp.einsum("tpo,pc->tco", out_terms, out_onehot, precision=lax.Precision.HIGHEST)
        hid_grad = jnp.einsum("trko,rkio->tri", grad_sel, w_out_wide)
        pre_grad = round_half(hid_grad * gelu_slope(preact))
        in_terms = jnp.einsum("tro,rkio->trki", pre_grad, w_in_wide).reshape(tok_total, pair_count, BLK)
        in_onehot = (in_flat[:, None] == columns[None, :]).astype(jnp.float32)
        in_total = in_total + jnp.einsum("tpi,pc->tci", in_terms, in_onehot, precision=lax.Precision.HIGHEST)
        group_in = jnp.einsum("gtrki,gtro->grkio", in_sel.reshape(N_DP, TOK, HB_DEV, KB, BLK), pre_grad.reshape(N_DP, TOK, HB_DEV, BLK))
        group_out = jnp.einsum("gtri,gtrko->grkio", hidden.reshape(N_DP, TOK, HB_DEV, BLK), grad_sel.reshape(N_DP, TOK, HB_DEV, KB, BLK))
        w_in_slab_grad = jnp.sum(round_half(group_in), axis=0).astype(jnp.bfloat16)
        w_out_slab_grad = jnp.sum(round_half(group_out), axis=0).astype(jnp.bfloat16)
        return (out_total, in_total), (w_in_slab_grad, w_out_slab_grad)

    start = jnp.zeros((tok_total, col_count, BLK), jnp.float32)
    totals, stacked = lax.scan(scan_step, (start, start), (w_in_group, in_group, w_out_group, out_group))
    outputs = totals[0].reshape(tok_total, D).astype(jnp.bfloat16)
    in_grad = totals[1].reshape(tok_total, D).astype(jnp.bfloat16)
    w_in_grad = stacked[0].reshape(N_MP * HB_DEV, KB, BLK, BLK)
    w_out_grad = stacked[1].reshape(N_MP * HB_DEV, KB, BLK, BLK)
    return (outputs, in_grad, w_in_grad, w_out_grad)
```

```python
import jax
import jax.numpy as jnp
from jax import lax
from jax.sharding import PartitionSpec as P

root_half = 0.7071067811865476
inv_root_two_pi = 0.3989422804014327


def gelu_value(preact):
    return 0.5 * preact * (1.0 + jax.scipy.special.erf(preact * root_half))


def gelu_slope(preact):
    return (
        0.5 * (1.0 + jax.scipy.special.erf(preact * root_half))
        + preact * jnp.exp(-0.5 * preact * preact) * inv_root_two_pi
    )


def per_device(inputs, out_grad, w_in, in_blocks, w_out, out_blocks):
    tok_rows = inputs.shape[0]
    hid_rows = w_in.shape[0]
    per_row = w_in.shape[1]
    block_size = w_in.shape[2]
    pair_count = hid_rows * per_row
    owners = lax.axis_size("mp")
    in_full, grad_full = (
        lax.all_gather(inputs, "mp", axis=1, tiled=True),
        lax.all_gather(out_grad, "mp", axis=1, tiled=True),
    )
    col_count = in_full.shape[1] // block_size
    in_flat = in_blocks.reshape(pair_count)
    out_flat = out_blocks.reshape(pair_count)
    empty = jnp.zeros((tok_rows, col_count, block_size), jnp.float32)
    in_sel = jnp.take(in_full.reshape(tok_rows, col_count, block_size), in_flat, axis=1)
    in_sel = in_sel.reshape(tok_rows, hid_rows, per_row, block_size)
    preact = jnp.einsum("trki,rkio->tro", in_sel, w_in, preferred_element_type=jnp.float32)
    hidden = gelu_value(preact).astype(jnp.bfloat16)
    out_terms = jnp.einsum("tri,rkio->trko", hidden, w_out, preferred_element_type=jnp.float32)
    out_terms = out_terms.reshape(tok_rows, pair_count, block_size)
    out_local = empty.at[:, out_flat].add(out_terms)
    out_local = out_local.reshape(tok_rows, col_count * block_size)

    def collect(received):
        received = received.reshape(owners, tok_rows, -1).astype(jnp.float32)
        return received.sum(axis=0).astype(jnp.bfloat16)

    def send_half(local):
        return lax.all_to_all(local.astype(jnp.bfloat16), "mp", split_axis=1, concat_axis=0, tiled=True)

    def dp_total(part):
        part = part.astype(jnp.bfloat16)
        if lax.axis_size("dp") == 2:
            other = lax.ppermute(part, "dp", perm=[(0, 1), (1, 0)])
            return (part.astype(jnp.float32) + other.astype(jnp.float32)).astype(jnp.bfloat16)
        return lax.psum(part, "dp")

    outputs = collect(send_half(out_local))
    grad_sel = jnp.take(grad_full.reshape(tok_rows, col_count, block_size), out_flat, axis=1)
    grad_sel = grad_sel.reshape(tok_rows, hid_rows, per_row, block_size)
    hid_grad = jnp.einsum("trko,rkio->tri", grad_sel, w_out, preferred_element_type=jnp.float32)
    pre_grad = (hid_grad * gelu_slope(preact)).astype(jnp.bfloat16)
    in_terms = jnp.einsum("tro,rkio->trki", pre_grad, w_in, preferred_element_type=jnp.float32)
    in_terms = in_terms.reshape(tok_rows, pair_count, block_size)
    in_local = empty.at[:, in_flat].add(in_terms)
    in_local = in_local.reshape(tok_rows, col_count * block_size)
    w_in_part = jnp.einsum("trki,tro->rkio", in_sel, pre_grad, preferred_element_type=jnp.float32)
    in_grad = collect(send_half(in_local))
    w_out_part = jnp.einsum("tri,trko->rkio", hidden, grad_sel, preferred_element_type=jnp.float32)
    w_in_grad = dp_total(w_in_part)
    w_out_grad = dp_total(w_out_part)
    return (outputs, in_grad, w_in_grad, w_out_grad)


def solution(mesh):
    return jax.shard_map(
        per_device,
        mesh=mesh,
        in_specs=(
            P("dp", "mp"),
            P("dp", "mp"),
            P("mp", None, None, None),
            P("mp", None),
            P("mp", None, None, None),
            P("mp", None),
        ),
        out_specs=(
            P("dp", "mp"),
            P("dp", "mp"),
            P("mp", None, None, None),
            P("mp", None, None, None),
        ),
        check_vma=False,
    )
```

```python
import jax
import jax.numpy as jnp
from jax import lax
from jax.sharding import PartitionSpec as P

root_half = 0.7071067811865476
inv_root_two_pi = 0.3989422804014327


def gelu_value(preact):
    return 0.5 * preact * (1.0 + jax.scipy.special.erf(preact * root_half))


def gelu_slope(preact):
    return (
        0.5 * (1.0 + jax.scipy.special.erf(preact * root_half))
        + preact * jnp.exp(-0.5 * preact * preact) * inv_root_two_pi
    )


def per_device(inputs, out_grad, w_in, in_blocks, w_out, out_blocks):
    tok_rows = inputs.shape[0]
    own_cols = inputs.shape[1]
    hid_rows = w_in.shape[0]
    per_row = w_in.shape[1]
    block_size = w_in.shape[2]
    pair_count = hid_rows * per_row
    owners = lax.axis_size("mp")
    own_blocks = own_cols // block_size
    col_count = owners * own_blocks

    both = jnp.concatenate([inputs, out_grad], axis=1)
    both = jnp.broadcast_to(both[None], (owners, tok_rows, 2 * own_cols))
    got = lax.all_to_all(both, "mp", split_axis=0, concat_axis=0, tiled=True)
    got = got.reshape(owners, tok_rows, 2, own_blocks, block_size)
    got = got.transpose(2, 1, 0, 3, 4).reshape(2, tok_rows, col_count, block_size)
    in_view, grad_view = got[0], got[1]

    in_flat = in_blocks.reshape(pair_count)
    out_flat = out_blocks.reshape(pair_count)
    columns = jnp.arange(col_count, dtype=jnp.int32)
    in_onehot = (in_flat[:, None] == columns[None, :]).astype(jnp.float32)
    out_onehot = (out_flat[:, None] == columns[None, :]).astype(jnp.float32)

    def dp_total(part):
        if lax.axis_size("dp") == 2:
            other = lax.ppermute(part, "dp", perm=[(0, 1), (1, 0)])
            return (part.astype(jnp.float32) + other.astype(jnp.float32)).astype(jnp.bfloat16)
        return lax.psum(part, "dp")

    def column_sums(terms, onehot):
        local = jnp.einsum("tpo,pc->cto", terms, onehot, precision=lax.Precision.HIGHEST,
                           preferred_element_type=jnp.float32)
        local = local.astype(jnp.bfloat16).reshape(owners, own_blocks * tok_rows * block_size)
        got = lax.all_to_all(local, "mp", split_axis=0, concat_axis=0, tiled=True)
        got = got.reshape(owners, own_blocks, tok_rows, block_size).astype(jnp.float32).sum(axis=0)
        return got.transpose(1, 0, 2).reshape(tok_rows, own_cols).astype(jnp.bfloat16)

    in_sel = jnp.take(in_view, in_flat, axis=1)
    in_sel = in_sel.reshape(tok_rows, hid_rows, per_row, block_size)
    grad_sel = jnp.take(grad_view, out_flat, axis=1)
    grad_sel = grad_sel.reshape(tok_rows, hid_rows, per_row, block_size)
    preact = jnp.einsum("trki,rkio->tro", in_sel, w_in, preferred_element_type=jnp.float32)
    hidden = gelu_value(preact).astype(jnp.bfloat16)

    w_out_part = jnp.einsum("tri,trko->rkio", hidden, grad_sel, preferred_element_type=jnp.float32)
    w_out_part = w_out_part.astype(jnp.bfloat16)
    w_out_part, hidden = lax.optimization_barrier((w_out_part, hidden))
    w_out_grad = dp_total(w_out_part)

    out_terms = jnp.einsum("tri,rkio->trko", hidden, w_out, preferred_element_type=jnp.float32)
    out_terms = out_terms.reshape(tok_rows, pair_count, block_size)
    outputs = column_sums(out_terms, out_onehot)

    hid_grad = jnp.einsum("trko,rkio->tri", grad_sel, w_out, preferred_element_type=jnp.float32)
    pre_grad = (hid_grad * gelu_slope(preact)).astype(jnp.bfloat16)

    w_in_part = jnp.einsum("trki,tro->rkio", in_sel, pre_grad, preferred_element_type=jnp.float32)
    w_in_part = w_in_part.astype(jnp.bfloat16)
    w_in_part, pre_grad = lax.optimization_barrier((w_in_part, pre_grad))
    w_in_grad = dp_total(w_in_part)

    in_terms = jnp.einsum("tro,rkio->trki", pre_grad, w_in, preferred_element_type=jnp.float32)
    in_terms = in_terms.reshape(tok_rows, pair_count, block_size)
    in_grad = column_sums(in_terms, in_onehot)
    return (outputs, in_grad, w_in_grad, w_out_grad)


def solution(mesh):
    return jax.shard_map(
        per_device,
        mesh=mesh,
        in_specs=(
            P("dp", "mp"),
            P("dp", "mp"),
            P("mp", None, None, None),
            P("mp", None),
            P("mp", None, None, None),
            P("mp", None),
        ),
        out_specs=(
            P("dp", "mp"),
            P("dp", "mp"),
            P("mp", None, None, None),
            P("mp", None, None, None),
        ),
        check_vma=False,
    )
```

```python
import jax
import jax.numpy as jnp
from jax import lax
from jax.sharding import Mesh, PartitionSpec as P

root_half = 0.7071067811865476
inv_root_two_pi = 0.3989422804014327


def gelu_value(preact):
    return 0.5 * preact * (1.0 + jax.scipy.special.erf(preact * root_half))


def gelu_slope(preact):
    return (
        0.5 * (1.0 + jax.scipy.special.erf(preact * root_half))
        + preact * jnp.exp(-0.5 * preact * preact) * inv_root_two_pi
    )


def swap_core(x):
    return lax.ppermute(x, "core", perm=[(0, 1), (1, 0)])


def per_device(inputs, out_grad, w_in, in_blocks, w_out, out_blocks):
    tok_rows = inputs.shape[0]
    own_cols = inputs.shape[1]
    hid_rows = w_in.shape[0]
    per_row = w_in.shape[1]
    block_size = w_in.shape[2]
    pair_count = hid_rows * per_row
    chips = lax.axis_size("chip")
    pair = lax.axis_size("core")
    own_blocks = own_cols // block_size
    col_count = chips * pair * own_blocks
    core = lax.axis_index("core")

    both = jnp.concatenate([inputs, out_grad], axis=1).reshape(tok_rows, 2, own_blocks, block_size)
    mine = lax.all_gather(both, "chip", axis=0, tiled=False)
    other = swap_core(mine)
    sets = jnp.stack([mine, other], axis=0)

    def select(flat, which):
        owner = flat // own_blocks
        sub = flat % own_blocks
        side = (owner % pair != core).astype(jnp.int32)
        sel = sets[side, owner // pair, :, which, sub, :]
        return sel.reshape(hid_rows, per_row, tok_rows, block_size)

    in_flat = in_blocks.reshape(pair_count)
    out_flat = out_blocks.reshape(pair_count)
    in_sel = select(in_flat, 0)
    grad_sel = select(out_flat, 1)

    def dp_total(part):
        part = part.astype(jnp.bfloat16)
        if lax.axis_size("dp") == 2:
            got = lax.ppermute(part, "dp", perm=[(0, 1), (1, 0)])
            return (part.astype(jnp.float32) + got.astype(jnp.float32)).astype(jnp.bfloat16)
        return lax.psum(part, "dp")

    empty = jnp.zeros((tok_rows, col_count, block_size), jnp.float32)

    def column_sums(terms, flat, tie=None):
        local = empty.at[:, flat].add(terms.reshape(tok_rows, pair_count, block_size))
        local = local.reshape(tok_rows, chips, pair, own_blocks, block_size)
        keep = lax.dynamic_index_in_dim(local, core, axis=2, keepdims=False)
        give = lax.dynamic_index_in_dim(local, 1 - core, axis=2, keepdims=False)
        chip_sum = (keep + swap_core(give)).astype(jnp.bfloat16)
        chip_sum = chip_sum.transpose(1, 0, 2, 3)
        if tie is not None:
            tie, chip_sum = lax.optimization_barrier((tie, chip_sum))
        got = lax.all_to_all(chip_sum, "chip", split_axis=0, concat_axis=0, tiled=True)
        total = got.astype(jnp.float32).sum(axis=0)
        return total.reshape(tok_rows, own_cols).astype(jnp.bfloat16), tie

    preact = jnp.einsum("rkti,rkio->tro", in_sel, w_in, preferred_element_type=jnp.float32)
    hidden = gelu_value(preact).astype(jnp.bfloat16)
    out_terms = jnp.einsum("tri,rkio->trko", hidden, w_out, preferred_element_type=jnp.float32)
    outputs, _ = column_sums(out_terms, out_flat)

    w_out_part = jnp.einsum("tri,rkto->rkio", hidden, grad_sel, preferred_element_type=jnp.float32)
    w_out_grad = dp_total(w_out_part)

    hid_grad = jnp.einsum("rkto,rkio->tri", grad_sel, w_out, preferred_element_type=jnp.float32)
    pre_grad = (hid_grad * gelu_slope(preact)).astype(jnp.bfloat16)
    in_terms = jnp.einsum("tro,rkio->trki", pre_grad, w_in, preferred_element_type=jnp.float32)
    in_grad, w_out_grad = column_sums(in_terms, in_flat, w_out_grad)
    w_in_part = jnp.einsum("rkti,tro->rkio", in_sel, pre_grad, preferred_element_type=jnp.float32)
    w_in_grad = dp_total(w_in_part)
    return (outputs, in_grad, w_in_grad, w_out_grad)


def solution(mesh):
    n_dp, n_mp = mesh.shape["dp"], mesh.shape["mp"]
    pair = 2 if n_mp % 2 == 0 else 1
    split = Mesh(mesh.devices.reshape(n_dp, n_mp // pair, pair), ("dp", "chip", "core"))
    cols = ("chip", "core")
    return jax.shard_map(
        per_device,
        mesh=split,
        in_specs=(
            P("dp", cols),
            P("dp", cols),
            P(cols, None, None, None),
            P(cols, None),
            P(cols, None, None, None),
            P(cols, None),
        ),
        out_specs=(
            P("dp", cols),
            P("dp", cols),
            P(cols, None, None, None),
            P(cols, None, None, None),
        ),
        check_vma=False,
    )
```

```python
import jax
import jax.numpy as jnp
from jax import lax
from jax.sharding import Mesh, PartitionSpec as P

root_half = 0.7071067811865476
inv_root_two_pi = 0.3989422804014327


def gelu_value(preact):
    return 0.5 * preact * (1.0 + jax.scipy.special.erf(preact * root_half))


def gelu_slope(preact):
    return (
        0.5 * (1.0 + jax.scipy.special.erf(preact * root_half))
        + preact * jnp.exp(-0.5 * preact * preact) * inv_root_two_pi
    )


def swap_core(x):
    return lax.ppermute(x, "core", perm=[(0, 1), (1, 0)])


def per_device(inputs, out_grad, w_in, in_blocks, w_out, out_blocks):
    tok_rows = inputs.shape[0]
    own_cols = inputs.shape[1]
    hid_rows = w_in.shape[0]
    per_row = w_in.shape[1]
    block_size = w_in.shape[2]
    pair_count = hid_rows * per_row
    chips = lax.axis_size("chip")
    pair = lax.axis_size("core")
    own_blocks = own_cols // block_size
    col_count = chips * pair * own_blocks
    core = lax.axis_index("core")

    both = jnp.concatenate([inputs, out_grad], axis=1).reshape(tok_rows, 2, own_blocks, block_size)
    mine = lax.all_gather(both, "chip", axis=0, tiled=False)
    other = swap_core(mine)
    sets = jnp.stack([mine, other], axis=0)

    def select(flat, which):
        owner = flat // own_blocks
        sub = flat % own_blocks
        side = (owner % pair != core).astype(jnp.int32)
        sel = sets[side, owner // pair, :, which, sub, :]
        return sel.reshape(hid_rows, per_row, tok_rows, block_size)

    in_flat = in_blocks.reshape(pair_count)
    out_flat = out_blocks.reshape(pair_count)
    in_sel = select(in_flat, 0)
    grad_sel = select(out_flat, 1)

    def dp_total(part):
        part = part.astype(jnp.bfloat16)
        if lax.axis_size("dp") == 2:
            got = lax.ppermute(part, "dp", perm=[(0, 1), (1, 0)])
            return (part.astype(jnp.float32) + got.astype(jnp.float32)).astype(jnp.bfloat16)
        return lax.psum(part, "dp")

    columns = jnp.arange(col_count, dtype=jnp.int32)

    def column_sums(terms, flat, tie=None):
        terms = terms.reshape(tok_rows, pair_count, block_size)
        hi = terms.astype(jnp.bfloat16)
        lo = (terms - hi.astype(jnp.float32)).astype(jnp.bfloat16)
        onehot = (flat[:, None] == columns[None, :]).astype(jnp.bfloat16)
        parts = jnp.concatenate([hi, lo], axis=1)
        picks = jnp.concatenate([onehot, onehot], axis=0)
        local = jnp.einsum("tpo,pc->cto", parts, picks, preferred_element_type=jnp.float32)
        local = local.reshape(chips, pair, own_blocks, tok_rows, block_size)
        keep = lax.dynamic_index_in_dim(local, core, axis=1, keepdims=False)
        give = lax.dynamic_index_in_dim(local, 1 - core, axis=1, keepdims=False)
        chip_sum = (keep + swap_core(give)).astype(jnp.bfloat16)
        if tie is not None:
            tie, chip_sum = lax.optimization_barrier((tie, chip_sum))
        got = lax.all_to_all(chip_sum, "chip", split_axis=0, concat_axis=0, tiled=True)
        total = got.astype(jnp.float32).sum(axis=0)
        return total.transpose(1, 0, 2).reshape(tok_rows, own_cols).astype(jnp.bfloat16), tie

    preact = jnp.einsum("rkti,rkio->tro", in_sel, w_in, preferred_element_type=jnp.float32)
    hidden = gelu_value(preact).astype(jnp.bfloat16)
    out_terms = jnp.einsum("tri,rkio->trko", hidden, w_out, preferred_element_type=jnp.float32)
    outputs, grad_sel = column_sums(out_terms, out_flat, grad_sel)

    w_out_part = jnp.einsum("tri,rkto->rkio", hidden, grad_sel, preferred_element_type=jnp.float32)
    w_out_grad = dp_total(w_out_part)

    hid_grad = jnp.einsum("rkto,rkio->tri", grad_sel, w_out, preferred_element_type=jnp.float32)
    pre_grad = (hid_grad * gelu_slope(preact)).astype(jnp.bfloat16)
    in_terms = jnp.einsum("tro,rkio->trki", pre_grad, w_in, preferred_element_type=jnp.float32)
    in_grad, w_out_grad = column_sums(in_terms, in_flat, w_out_grad)
    w_in_part = jnp.einsum("rkti,tro->rkio", in_sel, pre_grad, preferred_element_type=jnp.float32)
    w_in_grad = dp_total(w_in_part)
    return (outputs, in_grad, w_in_grad, w_out_grad)


def solution(mesh):
    n_dp, n_mp = mesh.shape["dp"], mesh.shape["mp"]
    pair = 2 if n_mp % 2 == 0 else 1
    split = Mesh(mesh.devices.reshape(n_dp, n_mp // pair, pair), ("dp", "chip", "core"))
    cols = ("chip", "core")
    return jax.shard_map(
        per_device,
        mesh=split,
        in_specs=(
            P("dp", cols),
            P("dp", cols),
            P(cols, None, None, None),
            P(cols, None),
            P(cols, None, None, None),
            P(cols, None),
        ),
        out_specs=(
            P("dp", cols),
            P("dp", cols),
            P(cols, None, None, None),
            P(cols, None, None, None),
        ),
        check_vma=False,
    )
```

```python
import jax
import jax.numpy as jnp
from jax import lax
from jax.sharding import Mesh, PartitionSpec as P

root_half = 0.7071067811865476
inv_root_two_pi = 0.3989422804014327


def gelu_value(preact):
    return 0.5 * preact * (1.0 + jax.scipy.special.erf(preact * root_half))


def gelu_slope(preact):
    return (
        0.5 * (1.0 + jax.scipy.special.erf(preact * root_half))
        + preact * jnp.exp(-0.5 * preact * preact) * inv_root_two_pi
    )


def swap_core(x):
    return lax.ppermute(x, "core", perm=[(0, 1), (1, 0)])


def per_device(inputs, out_grad, w_in, in_blocks, w_out, out_blocks):
    tok_rows = inputs.shape[0]
    own_cols = inputs.shape[1]
    hid_rows = w_in.shape[0]
    per_row = w_in.shape[1]
    block_size = w_in.shape[2]
    pair_count = hid_rows * per_row
    chips = lax.axis_size("chip")
    pair = lax.axis_size("core")
    own_blocks = own_cols // block_size
    col_count = chips * pair * own_blocks
    core = lax.axis_index("core")

    def gather(x):
        x = x.reshape(tok_rows, own_blocks, block_size)
        mine = lax.all_gather(x, "chip", axis=0, tiled=False)
        return jnp.stack([mine, swap_core(mine)], axis=0)

    def select(sets, flat):
        owner = flat // own_blocks
        sub = flat % own_blocks
        side = (owner % pair != core).astype(jnp.int32)
        sel = sets[side, owner // pair, :, sub, :]
        return sel.reshape(hid_rows, per_row, tok_rows, block_size)

    in_flat = in_blocks.reshape(pair_count)
    out_flat = out_blocks.reshape(pair_count)
    in_sel = select(gather(inputs), in_flat)
    grad_sel = select(gather(out_grad), out_flat)

    def dp_total(part):
        part = part.astype(jnp.bfloat16)
        if lax.axis_size("dp") == 2:
            got = lax.ppermute(part, "dp", perm=[(0, 1), (1, 0)])
            return (part.astype(jnp.float32) + got.astype(jnp.float32)).astype(jnp.bfloat16)
        return lax.psum(part, "dp")

    columns = jnp.arange(col_count, dtype=jnp.int32)

    def column_sums(terms, flat, tie=None):
        terms = terms.reshape(tok_rows, pair_count, block_size)
        hi = terms.astype(jnp.bfloat16)
        lo = (terms - hi.astype(jnp.float32)).astype(jnp.bfloat16)
        onehot = (flat[:, None] == columns[None, :]).astype(jnp.bfloat16)
        parts = jnp.concatenate([hi, lo], axis=1)
        picks = jnp.concatenate([onehot, onehot], axis=0)
        local = jnp.einsum("tpo,pc->cto", parts, picks, preferred_element_type=jnp.float32)
        local = local.reshape(chips, pair, own_blocks, tok_rows, block_size)
        keep = lax.dynamic_index_in_dim(local, core, axis=1, keepdims=False)
        give = lax.dynamic_index_in_dim(local, 1 - core, axis=1, keepdims=False)
        chip_sum = (keep + swap_core(give)).astype(jnp.bfloat16)
        if tie is not None:
            tie, chip_sum = lax.optimization_barrier((tie, chip_sum))
        got = lax.all_to_all(chip_sum, "chip", split_axis=0, concat_axis=0, tiled=True)
        total = got.astype(jnp.float32).sum(axis=0)
        return total.transpose(1, 0, 2).reshape(tok_rows, own_cols).astype(jnp.bfloat16), tie

    preact = jnp.einsum("rkti,rkio->tro", in_sel, w_in, preferred_element_type=jnp.float32)
    hidden = gelu_value(preact).astype(jnp.bfloat16)
    out_terms = jnp.einsum("tri,rkio->trko", hidden, w_out, preferred_element_type=jnp.float32)
    outputs, grad_sel = column_sums(out_terms, out_flat, grad_sel)

    w_out_part = jnp.einsum("tri,rkto->rkio", hidden, grad_sel, preferred_element_type=jnp.float32)
    w_out_grad = dp_total(w_out_part)

    hid_grad = jnp.einsum("rkto,rkio->tri", grad_sel, w_out, preferred_element_type=jnp.float32)
    pre_grad = (hid_grad * gelu_slope(preact)).astype(jnp.bfloat16)
    in_terms = jnp.einsum("tro,rkio->trki", pre_grad, w_in, preferred_element_type=jnp.float32)
    in_grad, w_out_grad = column_sums(in_terms, in_flat, w_out_grad)
    w_in_part = jnp.einsum("rkti,tro->rkio", in_sel, pre_grad, preferred_element_type=jnp.float32)
    w_in_grad = dp_total(w_in_part)
    return (outputs, in_grad, w_in_grad, w_out_grad)


def solution(mesh):
    n_dp, n_mp = mesh.shape["dp"], mesh.shape["mp"]
    pair = 2 if n_mp % 2 == 0 else 1
    split = Mesh(mesh.devices.reshape(n_dp, n_mp // pair, pair), ("dp", "chip", "core"))
    cols = ("chip", "core")
    return jax.shard_map(
        per_device,
        mesh=split,
        in_specs=(
            P("dp", cols),
            P("dp", cols),
            P(cols, None, None, None),
            P(cols, None),
            P(cols, None, None, None),
            P(cols, None),
        ),
        out_specs=(
            P("dp", cols),
            P("dp", cols),
            P(cols, None, None, None),
            P(cols, None, None, None),
        ),
        check_vma=False,
    )
```

```python
import jax
import jax.numpy as jnp
from jax import lax
from jax.sharding import Mesh, PartitionSpec as P

root_half = 0.7071067811865476
inv_root_two_pi = 0.3989422804014327


def gelu_value(preact):
    return 0.5 * preact * (1.0 + jax.scipy.special.erf(preact * root_half))


def gelu_slope(preact):
    return (
        0.5 * (1.0 + jax.scipy.special.erf(preact * root_half))
        + preact * jnp.exp(-0.5 * preact * preact) * inv_root_two_pi
    )


def swap_core(x):
    return lax.ppermute(x, "core", perm=[(0, 1), (1, 0)])


def per_device(inputs, out_grad, w_in, in_blocks, w_out, out_blocks):
    tok_rows = inputs.shape[0]
    own_cols = inputs.shape[1]
    hid_rows = w_in.shape[0]
    per_row = w_in.shape[1]
    block_size = w_in.shape[2]
    pair_count = hid_rows * per_row
    chips = lax.axis_size("chip")
    pair = lax.axis_size("core")
    own_blocks = own_cols // block_size
    col_count = chips * pair * own_blocks
    core = lax.axis_index("core")

    both = jnp.concatenate([inputs, out_grad], axis=1).reshape(tok_rows, 2, own_blocks, block_size)
    mine = lax.all_gather(both, "chip", axis=0, tiled=False)
    other = swap_core(mine)
    sets = jnp.stack([mine, other], axis=0)

    def select(flat, which):
        owner = flat // own_blocks
        sub = flat % own_blocks
        side = (owner % pair != core).astype(jnp.int32)
        sel = sets[side, owner // pair, :, which, sub, :]
        return sel.reshape(hid_rows, per_row, tok_rows, block_size)

    in_flat = in_blocks.reshape(pair_count)
    out_flat = out_blocks.reshape(pair_count)
    in_sel = select(in_flat, 0)
    grad_sel = select(out_flat, 1)

    def dp_total(part):
        part = part.astype(jnp.bfloat16)
        if lax.axis_size("dp") == 2:
            got = lax.ppermute(part, "dp", perm=[(0, 1), (1, 0)])
            return (part.astype(jnp.float32) + got.astype(jnp.float32)).astype(jnp.bfloat16)
        return lax.psum(part, "dp")

    columns = jnp.arange(col_count, dtype=jnp.int32)

    def chip_sums(terms, flat):
        terms = terms.reshape(tok_rows, pair_count, block_size)
        hi = terms.astype(jnp.bfloat16)
        lo = (terms - hi.astype(jnp.float32)).astype(jnp.bfloat16)
        onehot = (flat[:, None] == columns[None, :]).astype(jnp.bfloat16)
        parts = jnp.concatenate([hi, lo], axis=1)
        picks = jnp.concatenate([onehot, onehot], axis=0)
        local = jnp.einsum("tpo,pc->cto", parts, picks, preferred_element_type=jnp.float32)
        local = local.reshape(chips, pair, own_blocks, tok_rows, block_size)
        keep = lax.dynamic_index_in_dim(local, core, axis=1, keepdims=False)
        give = lax.dynamic_index_in_dim(local, 1 - core, axis=1, keepdims=False)
        return (keep + swap_core(give)).astype(jnp.bfloat16)

    def finish(got):
        total = got.astype(jnp.float32).sum(axis=0)
        return total.transpose(1, 0, 2).reshape(tok_rows, own_cols).astype(jnp.bfloat16)

    preact = jnp.einsum("rkti,rkio->tro", in_sel, w_in, preferred_element_type=jnp.float32)
    hidden = gelu_value(preact).astype(jnp.bfloat16)
    out_terms = jnp.einsum("tri,rkio->trko", hidden, w_out, preferred_element_type=jnp.float32)
    out_send = chip_sums(out_terms, out_flat)

    w_out_part = jnp.einsum("tri,rkto->rkio", hidden, grad_sel, preferred_element_type=jnp.float32)
    w_out_grad = dp_total(w_out_part)

    hid_grad = jnp.einsum("rkto,rkio->tri", grad_sel, w_out, preferred_element_type=jnp.float32)
    pre_grad = (hid_grad * gelu_slope(preact)).astype(jnp.bfloat16)
    in_terms = jnp.einsum("tro,rkio->trki", pre_grad, w_in, preferred_element_type=jnp.float32)
    in_send = chip_sums(in_terms, in_flat)
    got = lax.all_to_all(jnp.stack([out_send, in_send], axis=1), "chip", split_axis=0, concat_axis=0, tiled=True)
    outputs = finish(got[:, 0])
    in_grad = finish(got[:, 1])
    w_in_part = jnp.einsum("rkti,tro->rkio", in_sel, pre_grad, preferred_element_type=jnp.float32)
    w_in_grad = dp_total(w_in_part)
    return (outputs, in_grad, w_in_grad, w_out_grad)


def solution(mesh):
    n_dp, n_mp = mesh.shape["dp"], mesh.shape["mp"]
    pair = 2 if n_mp % 2 == 0 else 1
    split = Mesh(mesh.devices.reshape(n_dp, n_mp // pair, pair), ("dp", "chip", "core"))
    cols = ("chip", "core")
    return jax.shard_map(
        per_device,
        mesh=split,
        in_specs=(
            P("dp", cols),
            P("dp", cols),
            P(cols, None, None, None),
            P(cols, None),
            P(cols, None, None, None),
            P(cols, None),
        ),
        out_specs=(
            P("dp", cols),
            P("dp", cols),
            P(cols, None, None, None),
            P(cols, None, None, None),
        ),
        check_vma=False,
    )
```

```python
import jax
import jax.numpy as jnp
from jax import lax
from jax.sharding import Mesh, PartitionSpec as P

root_half = 0.7071067811865476
inv_root_two_pi = 0.3989422804014327


def gelu_value(preact):
    return 0.5 * preact * (1.0 + jax.scipy.special.erf(preact * root_half))


def gelu_slope(preact):
    return (
        0.5 * (1.0 + jax.scipy.special.erf(preact * root_half))
        + preact * jnp.exp(-0.5 * preact * preact) * inv_root_two_pi
    )


def per_device(inputs, out_grad, w_in, in_blocks, w_out, out_blocks):
    tok_rows = inputs.shape[0]
    own_cols = inputs.shape[1]
    hid_rows = w_in.shape[0]
    per_row = w_in.shape[1]
    block_size = w_in.shape[2]
    pair_count = hid_rows * per_row
    halves = lax.axis_size("zh")
    mids = lax.axis_size("mid")
    pair = lax.axis_size("core")
    own_blocks = own_cols // block_size
    col_count = halves * mids * pair * own_blocks
    core = lax.axis_index("core")
    half = lax.axis_index("zh")

    def swap(x, axis):
        return lax.ppermute(x, axis, perm=[(0, 1), (1, 0)])

    both = jnp.concatenate([inputs, out_grad], axis=1).reshape(tok_rows, 2, own_blocks, block_size)
    near = jnp.stack([both, swap(both, "zh")], axis=0)
    mine = lax.all_gather(near, "mid", axis=0, tiled=False)
    sets = jnp.stack([mine, swap(mine, "core")], axis=0)

    def select(flat, which):
        owner = flat // own_blocks
        sub = flat % own_blocks
        chip = owner // pair
        core_side = (owner % pair != core).astype(jnp.int32)
        half_side = (chip // mids != half).astype(jnp.int32)
        sel = sets[core_side, chip % mids, half_side, :, which, sub, :]
        return sel.reshape(hid_rows, per_row, tok_rows, block_size)

    in_flat = in_blocks.reshape(pair_count)
    out_flat = out_blocks.reshape(pair_count)
    in_sel = select(in_flat, 0)
    grad_sel = select(out_flat, 1)

    def dp_total(part):
        part = part.astype(jnp.bfloat16)
        if lax.axis_size("dp") == 2:
            got = lax.ppermute(part, "dp", perm=[(0, 1), (1, 0)])
            return (part.astype(jnp.float32) + got.astype(jnp.float32)).astype(jnp.bfloat16)
        return lax.psum(part, "dp")

    columns = jnp.arange(col_count, dtype=jnp.int32)

    def chip_sums(terms, flat):
        terms = terms.reshape(tok_rows, pair_count, block_size)
        hi = terms.astype(jnp.bfloat16)
        lo = (terms - hi.astype(jnp.float32)).astype(jnp.bfloat16)
        onehot = (flat[:, None] == columns[None, :]).astype(jnp.bfloat16)
        parts = jnp.concatenate([hi, lo], axis=1)
        picks = jnp.concatenate([onehot, onehot], axis=0)
        local = jnp.einsum("tpo,pc->cto", parts, picks, preferred_element_type=jnp.float32)
        local = local.reshape(halves, mids, pair, own_blocks, tok_rows, block_size)
        keep = lax.dynamic_index_in_dim(local, core, axis=2, keepdims=False)
        give = lax.dynamic_index_in_dim(local, 1 - core, axis=2, keepdims=False)
        return (keep + swap(give, "core")).astype(jnp.bfloat16)

    def finish(total):
        return total.transpose(1, 0, 2).reshape(tok_rows, own_cols).astype(jnp.bfloat16)

    preact = jnp.einsum("rkti,rkio->tro", in_sel, w_in, preferred_element_type=jnp.float32)
    hidden = gelu_value(preact).astype(jnp.bfloat16)
    out_terms = jnp.einsum("tri,rkio->trko", hidden, w_out, preferred_element_type=jnp.float32)
    out_send = chip_sums(out_terms, out_flat)

    w_out_part = jnp.einsum("tri,rkto->rkio", hidden, grad_sel, preferred_element_type=jnp.float32)
    w_out_grad = dp_total(w_out_part)

    hid_grad = jnp.einsum("rkto,rkio->tri", grad_sel, w_out, preferred_element_type=jnp.float32)
    pre_grad = (hid_grad * gelu_slope(preact)).astype(jnp.bfloat16)
    in_terms = jnp.einsum("tro,rkio->trki", pre_grad, w_in, preferred_element_type=jnp.float32)
    in_send = chip_sums(in_terms, in_flat)
    send = jnp.stack([out_send, in_send], axis=2)
    got = lax.all_to_all(send, "mid", split_axis=1, concat_axis=1, tiled=True)
    half_sum = got.astype(jnp.float32).sum(axis=1).astype(jnp.bfloat16)
    keep = lax.dynamic_index_in_dim(half_sum, half, axis=0, keepdims=False)
    give = lax.dynamic_index_in_dim(half_sum, 1 - half, axis=0, keepdims=False)
    total = keep.astype(jnp.float32) + swap(give, "zh").astype(jnp.float32)
    outputs = finish(total[0])
    in_grad = finish(total[1])
    w_in_part = jnp.einsum("rkti,tro->rkio", in_sel, pre_grad, preferred_element_type=jnp.float32)
    w_in_grad = dp_total(w_in_part)
    return (outputs, in_grad, w_in_grad, w_out_grad)


def solution(mesh):
    n_dp, n_mp = mesh.shape["dp"], mesh.shape["mp"]
    split = Mesh(mesh.devices.reshape(n_dp, 2, n_mp // 4, 2), ("dp", "zh", "mid", "core"))
    cols = ("zh", "mid", "core")
    return jax.shard_map(
        per_device,
        mesh=split,
        in_specs=(
            P("dp", cols),
            P("dp", cols),
            P(cols, None, None, None),
            P(cols, None),
            P(cols, None, None, None),
            P(cols, None),
        ),
        out_specs=(
            P("dp", cols),
            P("dp", cols),
            P(cols, None, None, None),
            P(cols, None, None, None),
        ),
        check_vma=False,
    )
```

```python
import jax
import jax.numpy as jnp
from jax import lax
from jax.sharding import Mesh, PartitionSpec as P

root_half = 0.7071067811865476
inv_root_two_pi = 0.3989422804014327


def gelu_value(preact):
    return 0.5 * preact * (1.0 + jax.scipy.special.erf(preact * root_half))


def gelu_slope(preact):
    return (
        0.5 * (1.0 + jax.scipy.special.erf(preact * root_half))
        + preact * jnp.exp(-0.5 * preact * preact) * inv_root_two_pi
    )


def swap_core(x):
    return lax.ppermute(x, "core", perm=[(0, 1), (1, 0)])


def per_device(inputs, out_grad, w_in, in_blocks, w_out, out_blocks):
    tok_rows = inputs.shape[0]
    own_cols = inputs.shape[1]
    hid_rows = w_in.shape[0]
    per_row = w_in.shape[1]
    block_size = w_in.shape[2]
    pair_count = hid_rows * per_row
    chips = lax.axis_size("chip")
    pair = lax.axis_size("core")
    own_blocks = own_cols // block_size
    col_count = chips * pair * own_blocks
    core = lax.axis_index("core")

    spread = jnp.broadcast_to(inputs.reshape(1, tok_rows, own_blocks, block_size), (chips, tok_rows, own_blocks, block_size))
    in_mine = lax.all_to_all(spread, "chip", split_axis=0, concat_axis=0, tiled=True)
    grad_mine = lax.all_gather(out_grad.reshape(tok_rows, own_blocks, block_size), "chip", axis=0, tiled=False)
    in_sets = jnp.stack([in_mine, swap_core(in_mine)], axis=0)
    grad_sets = jnp.stack([grad_mine, swap_core(grad_mine)], axis=0)

    def select(sets, flat):
        owner = flat // own_blocks
        sub = flat % own_blocks
        side = (owner % pair != core).astype(jnp.int32)
        sel = sets[side, owner // pair, :, sub, :]
        return sel.reshape(hid_rows, per_row, tok_rows, block_size)

    in_flat = in_blocks.reshape(pair_count)
    out_flat = out_blocks.reshape(pair_count)
    in_sel = select(in_sets, in_flat)
    grad_sel = select(grad_sets, out_flat)

    def dp_total(part):
        part = part.astype(jnp.bfloat16)
        if lax.axis_size("dp") == 2:
            got = lax.ppermute(part, "dp", perm=[(0, 1), (1, 0)])
            return (part.astype(jnp.float32) + got.astype(jnp.float32)).astype(jnp.bfloat16)
        return lax.psum(part, "dp")

    columns = jnp.arange(col_count, dtype=jnp.int32)

    def chip_sums(terms, flat):
        terms = terms.reshape(tok_rows, pair_count, block_size)
        hi = terms.astype(jnp.bfloat16)
        lo = (terms - hi.astype(jnp.float32)).astype(jnp.bfloat16)
        onehot = (flat[:, None] == columns[None, :]).astype(jnp.bfloat16)
        parts = jnp.concatenate([hi, lo], axis=1)
        picks = jnp.concatenate([onehot, onehot], axis=0)
        local = jnp.einsum("tpo,pc->cto", parts, picks, preferred_element_type=jnp.float32)
        local = local.reshape(chips, pair, own_blocks, tok_rows, block_size)
        keep = lax.dynamic_index_in_dim(local, core, axis=1, keepdims=False)
        give = lax.dynamic_index_in_dim(local, 1 - core, axis=1, keepdims=False)
        return (keep + swap_core(give)).astype(jnp.bfloat16)

    def finish(got):
        total = got.astype(jnp.float32).sum(axis=0)
        return total.transpose(1, 0, 2).reshape(tok_rows, own_cols).astype(jnp.bfloat16)

    preact = jnp.einsum("rkti,rkio->tro", in_sel, w_in, preferred_element_type=jnp.float32)
    hidden = gelu_value(preact).astype(jnp.bfloat16)
    out_terms = jnp.einsum("tri,rkio->trko", hidden, w_out, preferred_element_type=jnp.float32)
    out_send = chip_sums(out_terms, out_flat)

    w_out_part = jnp.einsum("tri,rkto->rkio", hidden, grad_sel, preferred_element_type=jnp.float32)
    w_out_grad = dp_total(w_out_part)

    hid_grad = jnp.einsum("rkto,rkio->tri", grad_sel, w_out, preferred_element_type=jnp.float32)
    pre_grad = (hid_grad * gelu_slope(preact)).astype(jnp.bfloat16)
    in_terms = jnp.einsum("tro,rkio->trki", pre_grad, w_in, preferred_element_type=jnp.float32)
    in_send = chip_sums(in_terms, in_flat)
    got = lax.all_to_all(jnp.stack([out_send, in_send], axis=1), "chip", split_axis=0, concat_axis=0, tiled=True)
    outputs = finish(got[:, 0])
    in_grad = finish(got[:, 1])
    w_in_part = jnp.einsum("rkti,tro->rkio", in_sel, pre_grad, preferred_element_type=jnp.float32)
    w_in_grad = dp_total(w_in_part)
    return (outputs, in_grad, w_in_grad, w_out_grad)


def solution(mesh):
    n_dp, n_mp = mesh.shape["dp"], mesh.shape["mp"]
    pair = 2 if n_mp % 2 == 0 else 1
    split = Mesh(mesh.devices.reshape(n_dp, n_mp // pair, pair), ("dp", "chip", "core"))
    cols = ("chip", "core")
    return jax.shard_map(
        per_device,
        mesh=split,
        in_specs=(
            P("dp", cols),
            P("dp", cols),
            P(cols, None, None, None),
            P(cols, None),
            P(cols, None, None, None),
            P(cols, None),
        ),
        out_specs=(
            P("dp", cols),
            P("dp", cols),
            P(cols, None, None, None),
            P(cols, None, None, None),
        ),
        check_vma=False,
    )
```

```python
import jax
import jax.numpy as jnp
from jax import lax
from jax.sharding import Mesh, PartitionSpec as P

root_half = 0.7071067811865476
inv_root_two_pi = 0.3989422804014327


def gelu_value(preact):
    return 0.5 * preact * (1.0 + jax.scipy.special.erf(preact * root_half))


def gelu_slope(preact):
    return (
        0.5 * (1.0 + jax.scipy.special.erf(preact * root_half))
        + preact * jnp.exp(-0.5 * preact * preact) * inv_root_two_pi
    )


def swap_core(x):
    return lax.ppermute(x, "core", perm=[(0, 1), (1, 0)])


def per_device(inputs, out_grad, w_in, in_blocks, w_out, out_blocks):
    tok_rows = inputs.shape[0]
    own_cols = inputs.shape[1]
    hid_rows = w_in.shape[0]
    per_row = w_in.shape[1]
    block_size = w_in.shape[2]
    pair_count = hid_rows * per_row
    chips = lax.axis_size("chip")
    pair = lax.axis_size("core")
    own_blocks = own_cols // block_size
    col_count = chips * pair * own_blocks
    core = lax.axis_index("core")

    both = jnp.concatenate([inputs, out_grad], axis=1).reshape(tok_rows, 2, own_blocks, block_size)
    mine = lax.all_gather(both, "chip", axis=0, tiled=False)
    other = swap_core(mine)
    sets = jnp.stack([mine, other], axis=0)

    def select(flat, which):
        owner = flat // own_blocks
        sub = flat % own_blocks
        side = (owner % pair != core).astype(jnp.int32)
        sel = sets[side, owner // pair, :, which, sub, :]
        return sel.reshape(hid_rows, per_row, tok_rows, block_size)

    in_flat = in_blocks.reshape(pair_count)
    out_flat = out_blocks.reshape(pair_count)
    in_sel = select(in_flat, 0)
    grad_sel = select(out_flat, 1)

    def dp_total(part):
        part = part.astype(jnp.bfloat16)
        if lax.axis_size("dp") == 2:
            got = lax.ppermute(part, "dp", perm=[(0, 1), (1, 0)])
            return (part.astype(jnp.float32) + got.astype(jnp.float32)).astype(jnp.bfloat16)
        return lax.psum(part, "dp")

    columns = jnp.arange(col_count, dtype=jnp.int32)

    def chip_sums(terms, flats):
        terms = terms.reshape(2, tok_rows, pair_count, block_size)
        hi = terms.astype(jnp.bfloat16)
        lo = (terms - hi.astype(jnp.float32)).astype(jnp.bfloat16)
        onehot = (flats[:, :, None] == columns[None, None, :]).astype(jnp.bfloat16)
        parts = jnp.concatenate([hi, lo], axis=2)
        picks = jnp.concatenate([onehot, onehot], axis=1)
        local = jnp.einsum("xtpo,xpc->cxto", parts, picks, preferred_element_type=jnp.float32)
        local = local.reshape(chips, pair, own_blocks, 2, tok_rows, block_size)
        keep = lax.dynamic_index_in_dim(local, core, axis=1, keepdims=False)
        give = lax.dynamic_index_in_dim(local, 1 - core, axis=1, keepdims=False)
        return (keep + swap_core(give)).astype(jnp.bfloat16)

    def finish(total):
        return total.transpose(1, 0, 2).reshape(tok_rows, own_cols).astype(jnp.bfloat16)

    preact = jnp.einsum("rkti,rkio->tro", in_sel, w_in, preferred_element_type=jnp.float32)
    hidden = gelu_value(preact).astype(jnp.bfloat16)
    out_terms = jnp.einsum("tri,rkio->trko", hidden, w_out, preferred_element_type=jnp.float32)

    w_out_part = jnp.einsum("tri,rkto->rkio", hidden, grad_sel, preferred_element_type=jnp.float32)
    w_out_grad = dp_total(w_out_part)

    hid_grad = jnp.einsum("rkto,rkio->tri", grad_sel, w_out, preferred_element_type=jnp.float32)
    pre_grad = (hid_grad * gelu_slope(preact)).astype(jnp.bfloat16)
    in_terms = jnp.einsum("tro,rkio->trki", pre_grad, w_in, preferred_element_type=jnp.float32)
    send = chip_sums(jnp.stack([out_terms, in_terms], axis=0), jnp.stack([out_flat, in_flat], axis=0))
    got = lax.all_to_all(send, "chip", split_axis=0, concat_axis=0, tiled=True)
    total = got.astype(jnp.float32).sum(axis=0)
    outputs = finish(total[:, 0])
    in_grad = finish(total[:, 1])
    w_in_part = jnp.einsum("rkti,tro->rkio", in_sel, pre_grad, preferred_element_type=jnp.float32)
    w_in_grad = dp_total(w_in_part)
    return (outputs, in_grad, w_in_grad, w_out_grad)


def solution(mesh):
    n_dp, n_mp = mesh.shape["dp"], mesh.shape["mp"]
    pair = 2 if n_mp % 2 == 0 else 1
    split = Mesh(mesh.devices.reshape(n_dp, n_mp // pair, pair), ("dp", "chip", "core"))
    cols = ("chip", "core")
    return jax.shard_map(
        per_device,
        mesh=split,
        in_specs=(
            P("dp", cols),
            P("dp", cols),
            P(cols, None, None, None),
            P(cols, None),
            P(cols, None, None, None),
            P(cols, None),
        ),
        out_specs=(
            P("dp", cols),
            P("dp", cols),
            P(cols, None, None, None),
            P(cols, None, None, None),
        ),
        check_vma=False,
    )
```

```python
import jax
import jax.numpy as jnp
from jax import lax
from jax.sharding import Mesh, PartitionSpec as P

root_half = 0.7071067811865476
inv_root_two_pi = 0.3989422804014327


def gelu_value(preact):
    return 0.5 * preact * (1.0 + jax.scipy.special.erf(preact * root_half))


def gelu_slope(preact):
    return (
        0.5 * (1.0 + jax.scipy.special.erf(preact * root_half))
        + preact * jnp.exp(-0.5 * preact * preact) * inv_root_two_pi
    )


def swap_core(x):
    return lax.ppermute(x, "core", perm=[(0, 1), (1, 0)])


def per_device(inputs, out_grad, w_in, in_blocks, w_out, out_blocks):
    tok_rows = inputs.shape[0]
    own_cols = inputs.shape[1]
    hid_rows = w_in.shape[0]
    per_row = w_in.shape[1]
    block_size = w_in.shape[2]
    pair_count = hid_rows * per_row
    chips = lax.axis_size("chip")
    pair = lax.axis_size("core")
    own_blocks = own_cols // block_size
    col_count = chips * pair * own_blocks
    core = lax.axis_index("core")

    both = jnp.concatenate([inputs, out_grad], axis=1).reshape(tok_rows, 2, own_blocks, block_size)
    both = both.transpose(1, 2, 0, 3)
    mine = lax.all_gather(both, "chip", axis=0, tiled=False)
    other = swap_core(mine)
    sets = jnp.stack([mine, other], axis=0)

    def select(flat, which):
        owner = flat // own_blocks
        sub = flat % own_blocks
        side = (owner % pair != core).astype(jnp.int32)
        sel = sets[side, owner // pair, which, sub]
        return sel.reshape(hid_rows, per_row, tok_rows, block_size)

    in_flat = in_blocks.reshape(pair_count)
    out_flat = out_blocks.reshape(pair_count)
    in_sel = select(in_flat, 0)
    grad_sel = select(out_flat, 1)

    def dp_total(part):
        part = part.astype(jnp.bfloat16)
        if lax.axis_size("dp") == 2:
            got = lax.ppermute(part, "dp", perm=[(0, 1), (1, 0)])
            return (part.astype(jnp.float32) + got.astype(jnp.float32)).astype(jnp.bfloat16)
        return lax.psum(part, "dp")

    columns = jnp.arange(col_count, dtype=jnp.int32)

    def chip_sums(terms, flat):
        terms = terms.reshape(tok_rows, pair_count, block_size)
        hi = terms.astype(jnp.bfloat16)
        lo = (terms - hi.astype(jnp.float32)).astype(jnp.bfloat16)
        onehot = (flat[:, None] == columns[None, :]).astype(jnp.bfloat16)
        parts = jnp.concatenate([hi, lo], axis=1)
        picks = jnp.concatenate([onehot, onehot], axis=0)
        local = jnp.einsum("tpo,pc->cto", parts, picks, preferred_element_type=jnp.float32)
        local = local.reshape(chips, pair, own_blocks, tok_rows, block_size)
        keep = lax.dynamic_index_in_dim(local, core, axis=1, keepdims=False)
        give = lax.dynamic_index_in_dim(local, 1 - core, axis=1, keepdims=False)
        return (keep + swap_core(give)).astype(jnp.bfloat16)

    def finish(got):
        total = got.astype(jnp.float32).sum(axis=0)
        return total.transpose(1, 0, 2).reshape(tok_rows, own_cols).astype(jnp.bfloat16)

    preact = jnp.einsum("rkti,rkio->tro", in_sel, w_in, preferred_element_type=jnp.float32)
    hidden = gelu_value(preact).astype(jnp.bfloat16)
    out_terms = jnp.einsum("tri,rkio->trko", hidden, w_out, preferred_element_type=jnp.float32)
    out_send = chip_sums(out_terms, out_flat)

    w_out_part = jnp.einsum("tri,rkto->rkio", hidden, grad_sel, preferred_element_type=jnp.float32)
    w_out_grad = dp_total(w_out_part)

    hid_grad = jnp.einsum("rkto,rkio->tri", grad_sel, w_out, preferred_element_type=jnp.float32)
    pre_grad = (hid_grad * gelu_slope(preact)).astype(jnp.bfloat16)
    in_terms = jnp.einsum("tro,rkio->trki", pre_grad, w_in, preferred_element_type=jnp.float32)
    in_send = chip_sums(in_terms, in_flat)
    got = lax.all_to_all(jnp.stack([out_send, in_send], axis=1), "chip", split_axis=0, concat_axis=0, tiled=True)
    outputs = finish(got[:, 0])
    in_grad = finish(got[:, 1])
    w_in_part = jnp.einsum("rkti,tro->rkio", in_sel, pre_grad, preferred_element_type=jnp.float32)
    w_in_grad = dp_total(w_in_part)
    return (outputs, in_grad, w_in_grad, w_out_grad)


def solution(mesh):
    n_dp, n_mp = mesh.shape["dp"], mesh.shape["mp"]
    pair = 2 if n_mp % 2 == 0 else 1
    split = Mesh(mesh.devices.reshape(n_dp, n_mp // pair, pair), ("dp", "chip", "core"))
    cols = ("chip", "core")
    return jax.shard_map(
        per_device,
        mesh=split,
        in_specs=(
            P("dp", cols),
            P("dp", cols),
            P(cols, None, None, None),
            P(cols, None),
            P(cols, None, None, None),
            P(cols, None),
        ),
        out_specs=(
            P("dp", cols),
            P("dp", cols),
            P(cols, None, None, None),
            P(cols, None, None, None),
        ),
        check_vma=False,
    )
```

```python
import jax
import jax.numpy as jnp
from jax import lax
from jax.sharding import Mesh, PartitionSpec as P

root_half = 0.7071067811865476
inv_root_two_pi = 0.3989422804014327


def gelu_value(preact):
    return 0.5 * preact * (1.0 + jax.scipy.special.erf(preact * root_half))


def gelu_slope(preact):
    return (
        0.5 * (1.0 + jax.scipy.special.erf(preact * root_half))
        + preact * jnp.exp(-0.5 * preact * preact) * inv_root_two_pi
    )


def swap_core(x):
    return lax.ppermute(x, "core", perm=[(0, 1), (1, 0)])


def per_device(inputs, out_grad, w_in, in_blocks, w_out, out_blocks):
    tok_rows = inputs.shape[0]
    own_cols = inputs.shape[1]
    hid_rows = w_in.shape[0]
    per_row = w_in.shape[1]
    block_size = w_in.shape[2]
    pair_count = hid_rows * per_row
    chips = lax.axis_size("chip")
    pair = lax.axis_size("core")
    own_blocks = own_cols // block_size
    col_count = chips * pair * own_blocks
    core = lax.axis_index("core")

    both = jnp.concatenate([inputs, out_grad], axis=1).reshape(tok_rows, 2, own_blocks, block_size)
    both = both.transpose(1, 2, 0, 3)
    mine = lax.all_gather(both, "chip", axis=0, tiled=False)
    other = swap_core(mine)
    chip_ids = jnp.arange(chips, dtype=jnp.int32)
    sub_ids = jnp.arange(own_blocks, dtype=jnp.int32)

    def select(flat, which):
        owner = flat // own_blocks
        sub = flat % own_blocks
        hit = (owner // pair)[:, None, None] == chip_ids[None, :, None]
        hit = hit & (sub[:, None, None] == sub_ids[None, None, :])
        here = (owner % pair == core)[:, None, None]
        near = (hit & here).astype(jnp.bfloat16)
        far = (hit & ~here).astype(jnp.bfloat16)
        sel = jnp.einsum("pcs,csto->pto", near, mine[:, which], preferred_element_type=jnp.float32)
        sel = sel + jnp.einsum("pcs,csto->pto", far, other[:, which], preferred_element_type=jnp.float32)
        return sel.astype(jnp.bfloat16).reshape(hid_rows, per_row, tok_rows, block_size)

    in_flat = in_blocks.reshape(pair_count)
    out_flat = out_blocks.reshape(pair_count)
    in_sel = select(in_flat, 0)
    grad_sel = select(out_flat, 1)

    def dp_total(part):
        part = part.astype(jnp.bfloat16)
        if lax.axis_size("dp") == 2:
            got = lax.ppermute(part, "dp", perm=[(0, 1), (1, 0)])
            return (part.astype(jnp.float32) + got.astype(jnp.float32)).astype(jnp.bfloat16)
        return lax.psum(part, "dp")

    columns = jnp.arange(col_count, dtype=jnp.int32)

    def chip_sums(terms, flat):
        terms = terms.reshape(tok_rows, pair_count, block_size)
        hi = terms.astype(jnp.bfloat16)
        lo = (terms - hi.astype(jnp.float32)).astype(jnp.bfloat16)
        onehot = (flat[:, None] == columns[None, :]).astype(jnp.bfloat16)
        parts = jnp.concatenate([hi, lo], axis=1)
        picks = jnp.concatenate([onehot, onehot], axis=0)
        local = jnp.einsum("tpo,pc->cto", parts, picks, preferred_element_type=jnp.float32)
        local = local.reshape(chips, pair, own_blocks, tok_rows, block_size)
        keep = lax.dynamic_index_in_dim(local, core, axis=1, keepdims=False)
        give = lax.dynamic_index_in_dim(local, 1 - core, axis=1, keepdims=False)
        return (keep + swap_core(give)).astype(jnp.bfloat16)

    def finish(got):
        total = got.astype(jnp.float32).sum(axis=0)
        return total.transpose(1, 0, 2).reshape(tok_rows, own_cols).astype(jnp.bfloat16)

    preact = jnp.einsum("rkti,rkio->tro", in_sel, w_in, preferred_element_type=jnp.float32)
    hidden = gelu_value(preact).astype(jnp.bfloat16)
    out_terms = jnp.einsum("tri,rkio->trko", hidden, w_out, preferred_element_type=jnp.float32)
    out_send = chip_sums(out_terms, out_flat)

    w_out_part = jnp.einsum("tri,rkto->rkio", hidden, grad_sel, preferred_element_type=jnp.float32)
    w_out_grad = dp_total(w_out_part)

    hid_grad = jnp.einsum("rkto,rkio->tri", grad_sel, w_out, preferred_element_type=jnp.float32)
    pre_grad = (hid_grad * gelu_slope(preact)).astype(jnp.bfloat16)
    in_terms = jnp.einsum("tro,rkio->trki", pre_grad, w_in, preferred_element_type=jnp.float32)
    in_send = chip_sums(in_terms, in_flat)
    got = lax.all_to_all(jnp.stack([out_send, in_send], axis=1), "chip", split_axis=0, concat_axis=0, tiled=True)
    outputs = finish(got[:, 0])
    in_grad = finish(got[:, 1])
    w_in_part = jnp.einsum("rkti,tro->rkio", in_sel, pre_grad, preferred_element_type=jnp.float32)
    w_in_grad = dp_total(w_in_part)
    return (outputs, in_grad, w_in_grad, w_out_grad)


def solution(mesh):
    n_dp, n_mp = mesh.shape["dp"], mesh.shape["mp"]
    pair = 2 if n_mp % 2 == 0 else 1
    split = Mesh(mesh.devices.reshape(n_dp, n_mp // pair, pair), ("dp", "chip", "core"))
    cols = ("chip", "core")
    return jax.shard_map(
        per_device,
        mesh=split,
        in_specs=(
            P("dp", cols),
            P("dp", cols),
            P(cols, None, None, None),
            P(cols, None),
            P(cols, None, None, None),
            P(cols, None),
        ),
        out_specs=(
            P("dp", cols),
            P("dp", cols),
            P(cols, None, None, None),
            P(cols, None, None, None),
        ),
        check_vma=False,
    )
```

```python
import jax
import jax.numpy as jnp
from jax import lax
from jax.sharding import Mesh, PartitionSpec as P

root_half = 0.7071067811865476
inv_root_two_pi = 0.3989422804014327


def gelu_value(preact):
    return 0.5 * preact * (1.0 + jax.scipy.special.erf(preact * root_half))


def gelu_slope(preact):
    return (
        0.5 * (1.0 + jax.scipy.special.erf(preact * root_half))
        + preact * jnp.exp(-0.5 * preact * preact) * inv_root_two_pi
    )


def swap_core(x):
    return lax.ppermute(x, "core", perm=[(0, 1), (1, 0)])


def gather_chips(x, chips):
    if chips & (chips - 1):
        return lax.all_gather(x, "chip", axis=0, tiled=False)
    me = lax.axis_index("chip")
    held = x[None]
    step = 1
    while step < chips:
        got = lax.ppermute(held, "chip", perm=[(i, i ^ step) for i in range(chips)])
        upper = (me // step) % 2 == 1
        held = jnp.where(upper, jnp.concatenate([got, held], axis=0), jnp.concatenate([held, got], axis=0))
        step *= 2
    return held


def per_device(inputs, out_grad, w_in, in_blocks, w_out, out_blocks):
    tok_rows = inputs.shape[0]
    own_cols = inputs.shape[1]
    hid_rows = w_in.shape[0]
    per_row = w_in.shape[1]
    block_size = w_in.shape[2]
    pair_count = hid_rows * per_row
    chips = lax.axis_size("chip")
    pair = lax.axis_size("core")
    own_blocks = own_cols // block_size
    col_count = chips * pair * own_blocks
    core = lax.axis_index("core")

    both = jnp.concatenate([inputs, out_grad], axis=1).reshape(tok_rows, 2, own_blocks, block_size)
    both = both.transpose(1, 2, 0, 3)
    mine = gather_chips(both, chips)
    other = swap_core(mine)
    sets = jnp.stack([mine, other], axis=0)

    def select(flat, which):
        owner = flat // own_blocks
        sub = flat % own_blocks
        side = (owner % pair != core).astype(jnp.int32)
        sel = sets[side, owner // pair, which, sub]
        return sel.reshape(hid_rows, per_row, tok_rows, block_size)

    in_flat = in_blocks.reshape(pair_count)
    out_flat = out_blocks.reshape(pair_count)
    in_sel = select(in_flat, 0)
    grad_sel = select(out_flat, 1)

    def dp_total(part):
        part = part.astype(jnp.bfloat16)
        if lax.axis_size("dp") == 2:
            got = lax.ppermute(part, "dp", perm=[(0, 1), (1, 0)])
            return (part.astype(jnp.float32) + got.astype(jnp.float32)).astype(jnp.bfloat16)
        return lax.psum(part, "dp")

    columns = jnp.arange(col_count, dtype=jnp.int32)

    def chip_sums(terms, flat):
        terms = terms.reshape(tok_rows, pair_count, block_size)
        hi = terms.astype(jnp.bfloat16)
        lo = (terms - hi.astype(jnp.float32)).astype(jnp.bfloat16)
        onehot = (flat[:, None] == columns[None, :]).astype(jnp.bfloat16)
        parts = jnp.concatenate([hi, lo], axis=1)
        picks = jnp.concatenate([onehot, onehot], axis=0)
        local = jnp.einsum("tpo,pc->cto", parts, picks, preferred_element_type=jnp.float32)
        local = local.reshape(chips, pair, own_blocks, tok_rows, block_size)
        keep = lax.dynamic_index_in_dim(local, core, axis=1, keepdims=False)
        give = lax.dynamic_index_in_dim(local, 1 - core, axis=1, keepdims=False)
        return (keep + swap_core(give)).astype(jnp.bfloat16)

    def finish(got):
        total = got.astype(jnp.float32).sum(axis=0)
        return total.transpose(1, 0, 2).reshape(tok_rows, own_cols).astype(jnp.bfloat16)

    preact = jnp.einsum("rkti,rkio->tro", in_sel, w_in, preferred_element_type=jnp.float32)
    hidden = gelu_value(preact).astype(jnp.bfloat16)
    out_terms = jnp.einsum("tri,rkio->trko", hidden, w_out, preferred_element_type=jnp.float32)
    out_send = chip_sums(out_terms, out_flat)

    w_out_part = jnp.einsum("tri,rkto->rkio", hidden, grad_sel, preferred_element_type=jnp.float32)
    w_out_grad = dp_total(w_out_part)

    hid_grad = jnp.einsum("rkto,rkio->tri", grad_sel, w_out, preferred_element_type=jnp.float32)
    pre_grad = (hid_grad * gelu_slope(preact)).astype(jnp.bfloat16)
    in_terms = jnp.einsum("tro,rkio->trki", pre_grad, w_in, preferred_element_type=jnp.float32)
    in_send = chip_sums(in_terms, in_flat)
    got = lax.all_to_all(jnp.stack([out_send, in_send], axis=1), "chip", split_axis=0, concat_axis=0, tiled=True)
    outputs = finish(got[:, 0])
    in_grad = finish(got[:, 1])
    w_in_part = jnp.einsum("rkti,tro->rkio", in_sel, pre_grad, preferred_element_type=jnp.float32)
    w_in_grad = dp_total(w_in_part)
    return (outputs, in_grad, w_in_grad, w_out_grad)


def solution(mesh):
    n_dp, n_mp = mesh.shape["dp"], mesh.shape["mp"]
    pair = 2 if n_mp % 2 == 0 else 1
    split = Mesh(mesh.devices.reshape(n_dp, n_mp // pair, pair), ("dp", "chip", "core"))
    cols = ("chip", "core")
    return jax.shard_map(
        per_device,
        mesh=split,
        in_specs=(
            P("dp", cols),
            P("dp", cols),
            P(cols, None, None, None),
            P(cols, None),
            P(cols, None, None, None),
            P(cols, None),
        ),
        out_specs=(
            P("dp", cols),
            P("dp", cols),
            P(cols, None, None, None),
            P(cols, None, None, None),
        ),
        check_vma=False,
    )
```

```python
import jax
import jax.numpy as jnp
from jax import lax
from jax.sharding import Mesh, PartitionSpec as P

root_half = 0.7071067811865476
inv_root_two_pi = 0.3989422804014327


def gelu_value(preact):
    return 0.5 * preact * (1.0 + jax.scipy.special.erf(preact * root_half))


def gelu_slope(preact):
    return (
        0.5 * (1.0 + jax.scipy.special.erf(preact * root_half))
        + preact * jnp.exp(-0.5 * preact * preact) * inv_root_two_pi
    )


def swap_core(x):
    return lax.ppermute(x, "core", perm=[(0, 1), (1, 0)])


def gather_chips(x, chips):
    if chips & (chips - 1):
        return lax.all_gather(x, "chip", axis=0, tiled=False)
    me = lax.axis_index("chip")
    held = x[None]
    step = chips // 2
    while step >= 1:
        got = lax.ppermute(held, "chip", perm=[(i, i ^ step) for i in range(chips)])
        upper = (me // step) % 2 == 1
        held = jnp.where(upper, jnp.concatenate([got, held], axis=0), jnp.concatenate([held, got], axis=0))
        step //= 2
    return held


def chip_slot(chip, chips):
    if chips & (chips - 1):
        return chip
    slot = jnp.zeros_like(chip)
    step = chips // 2
    while step >= 1:
        slot = slot + ((chip // step) % 2) * (chips // (2 * step))
        step //= 2
    return slot


def per_device(inputs, out_grad, w_in, in_blocks, w_out, out_blocks):
    tok_rows = inputs.shape[0]
    own_cols = inputs.shape[1]
    hid_rows = w_in.shape[0]
    per_row = w_in.shape[1]
    block_size = w_in.shape[2]
    pair_count = hid_rows * per_row
    chips = lax.axis_size("chip")
    pair = lax.axis_size("core")
    own_blocks = own_cols // block_size
    col_count = chips * pair * own_blocks
    core = lax.axis_index("core")

    both = jnp.concatenate([inputs, out_grad], axis=1).reshape(tok_rows, 2, own_blocks, block_size)
    both = both.transpose(1, 2, 0, 3)
    mine = gather_chips(both, chips)
    other = swap_core(mine)
    sets = jnp.stack([mine, other], axis=0)

    def select(flat, which):
        owner = flat // own_blocks
        sub = flat % own_blocks
        side = (owner % pair != core).astype(jnp.int32)
        sel = sets[side, chip_slot(owner // pair, chips), which, sub]
        return sel.reshape(hid_rows, per_row, tok_rows, block_size)

    in_flat = in_blocks.reshape(pair_count)
    out_flat = out_blocks.reshape(pair_count)
    in_sel = select(in_flat, 0)
    grad_sel = select(out_flat, 1)

    def dp_total(part):
        part = part.astype(jnp.bfloat16)
        if lax.axis_size("dp") == 2:
            got = lax.ppermute(part, "dp", perm=[(0, 1), (1, 0)])
            return (part.astype(jnp.float32) + got.astype(jnp.float32)).astype(jnp.bfloat16)
        return lax.psum(part, "dp")

    columns = jnp.arange(col_count, dtype=jnp.int32)

    def chip_sums(terms, flat):
        terms = terms.reshape(tok_rows, pair_count, block_size)
        hi = terms.astype(jnp.bfloat16)
        lo = (terms - hi.astype(jnp.float32)).astype(jnp.bfloat16)
        onehot = (flat[:, None] == columns[None, :]).astype(jnp.bfloat16)
        parts = jnp.concatenate([hi, lo], axis=1)
        picks = jnp.concatenate([onehot, onehot], axis=0)
        local = jnp.einsum("tpo,pc->cto", parts, picks, preferred_element_type=jnp.float32)
        local = local.reshape(chips, pair, own_blocks, tok_rows, block_size)
        keep = lax.dynamic_index_in_dim(local, core, axis=1, keepdims=False)
        give = lax.dynamic_index_in_dim(local, 1 - core, axis=1, keepdims=False)
        return (keep + swap_core(give)).astype(jnp.bfloat16)

    def finish(got):
        total = got.astype(jnp.float32).sum(axis=0)
        return total.transpose(1, 0, 2).reshape(tok_rows, own_cols).astype(jnp.bfloat16)

    preact = jnp.einsum("rkti,rkio->tro", in_sel, w_in, preferred_element_type=jnp.float32)
    hidden = gelu_value(preact).astype(jnp.bfloat16)
    out_terms = jnp.einsum("tri,rkio->trko", hidden, w_out, preferred_element_type=jnp.float32)
    out_send = chip_sums(out_terms, out_flat)

    w_out_part = jnp.einsum("tri,rkto->rkio", hidden, grad_sel, preferred_element_type=jnp.float32)
    w_out_grad = dp_total(w_out_part)

    hid_grad = jnp.einsum("rkto,rkio->tri", grad_sel, w_out, preferred_element_type=jnp.float32)
    pre_grad = (hid_grad * gelu_slope(preact)).astype(jnp.bfloat16)
    in_terms = jnp.einsum("tro,rkio->trki", pre_grad, w_in, preferred_element_type=jnp.float32)
    in_send = chip_sums(in_terms, in_flat)
    got = lax.all_to_all(jnp.stack([out_send, in_send], axis=1), "chip", split_axis=0, concat_axis=0, tiled=True)
    outputs = finish(got[:, 0])
    in_grad = finish(got[:, 1])
    w_in_part = jnp.einsum("rkti,tro->rkio", in_sel, pre_grad, preferred_element_type=jnp.float32)
    w_in_grad = dp_total(w_in_part)
    return (outputs, in_grad, w_in_grad, w_out_grad)


def solution(mesh):
    n_dp, n_mp = mesh.shape["dp"], mesh.shape["mp"]
    pair = 2 if n_mp % 2 == 0 else 1
    split = Mesh(mesh.devices.reshape(n_dp, n_mp // pair, pair), ("dp", "chip", "core"))
    cols = ("chip", "core")
    return jax.shard_map(
        per_device,
        mesh=split,
        in_specs=(
            P("dp", cols),
            P("dp", cols),
            P(cols, None, None, None),
            P(cols, None),
            P(cols, None, None, None),
            P(cols, None),
        ),
        out_specs=(
            P("dp", cols),
            P("dp", cols),
            P(cols, None, None, None),
            P(cols, None, None, None),
        ),
        check_vma=False,
    )
```

```python
import jax
import jax.numpy as jnp
from jax import lax
from jax.sharding import Mesh, PartitionSpec as P

root_half = 0.7071067811865476
inv_root_two_pi = 0.3989422804014327


def gelu_value(preact):
    return 0.5 * preact * (1.0 + jax.scipy.special.erf(preact * root_half))


def gelu_slope(preact):
    return (
        0.5 * (1.0 + jax.scipy.special.erf(preact * root_half))
        + preact * jnp.exp(-0.5 * preact * preact) * inv_root_two_pi
    )


def swap_core(x):
    return lax.ppermute(x, "core", perm=[(0, 1), (1, 0)])


def chip_orders(chips):
    if chips & (chips - 1) or chips < 2:
        return None, None
    steps = []
    step = chips // 2
    while step >= 1:
        steps.append(step)
        step //= 2
    return steps, steps[:1] + steps[1:][::-1]


def gather_chips(x, chips, order):
    if order is None:
        return lax.all_gather(x, "chip", axis=0, tiled=False)
    me = lax.axis_index("chip")
    held = x[None]
    for step in order:
        got = lax.ppermute(held, "chip", perm=[(i, i ^ step) for i in range(chips)])
        upper = (me // step) % 2 == 1
        held = jnp.where(upper, jnp.concatenate([got, held], axis=0), jnp.concatenate([held, got], axis=0))
    return held


def chip_slot(chip, order):
    if order is None:
        return chip
    slot = jnp.zeros_like(chip)
    for k, step in enumerate(order):
        slot = slot + ((chip // step) % 2) * (1 << k)
    return slot


def per_device(inputs, out_grad, w_in, in_blocks, w_out, out_blocks):
    tok_rows = inputs.shape[0]
    own_cols = inputs.shape[1]
    hid_rows = w_in.shape[0]
    per_row = w_in.shape[1]
    block_size = w_in.shape[2]
    pair_count = hid_rows * per_row
    chips = lax.axis_size("chip")
    pair = lax.axis_size("core")
    own_blocks = own_cols // block_size
    col_count = chips * pair * own_blocks
    core = lax.axis_index("core")

    order_in, order_grad = chip_orders(chips)

    def gather(x, order):
        x = x.reshape(tok_rows, own_blocks, block_size).transpose(1, 0, 2)
        mine = gather_chips(x, chips, order)
        return jnp.stack([mine, swap_core(mine)], axis=0)

    def select(sets, flat, order):
        owner = flat // own_blocks
        sub = flat % own_blocks
        side = (owner % pair != core).astype(jnp.int32)
        sel = sets[side, chip_slot(owner // pair, order), sub]
        return sel.reshape(hid_rows, per_row, tok_rows, block_size)

    in_flat = in_blocks.reshape(pair_count)
    out_flat = out_blocks.reshape(pair_count)
    in_sel = select(gather(inputs, order_in), in_flat, order_in)
    grad_sel = select(gather(out_grad, order_grad), out_flat, order_grad)

    def dp_total(part):
        part = part.astype(jnp.bfloat16)
        if lax.axis_size("dp") == 2:
            got = lax.ppermute(part, "dp", perm=[(0, 1), (1, 0)])
            return (part.astype(jnp.float32) + got.astype(jnp.float32)).astype(jnp.bfloat16)
        return lax.psum(part, "dp")

    columns = jnp.arange(col_count, dtype=jnp.int32)

    def chip_sums(terms, flat):
        terms = terms.reshape(tok_rows, pair_count, block_size)
        hi = terms.astype(jnp.bfloat16)
        lo = (terms - hi.astype(jnp.float32)).astype(jnp.bfloat16)
        onehot = (flat[:, None] == columns[None, :]).astype(jnp.bfloat16)
        parts = jnp.concatenate([hi, lo], axis=1)
        picks = jnp.concatenate([onehot, onehot], axis=0)
        local = jnp.einsum("tpo,pc->cto", parts, picks, preferred_element_type=jnp.float32)
        local = local.reshape(chips, pair, own_blocks, tok_rows, block_size)
        keep = lax.dynamic_index_in_dim(local, core, axis=1, keepdims=False)
        give = lax.dynamic_index_in_dim(local, 1 - core, axis=1, keepdims=False)
        return (keep + swap_core(give)).astype(jnp.bfloat16)

    def finish(got):
        total = got.astype(jnp.float32).sum(axis=0)
        return total.transpose(1, 0, 2).reshape(tok_rows, own_cols).astype(jnp.bfloat16)

    preact = jnp.einsum("rkti,rkio->tro", in_sel, w_in, preferred_element_type=jnp.float32)
    hidden = gelu_value(preact).astype(jnp.bfloat16)
    out_terms = jnp.einsum("tri,rkio->trko", hidden, w_out, preferred_element_type=jnp.float32)
    out_send = chip_sums(out_terms, out_flat)

    w_out_part = jnp.einsum("tri,rkto->rkio", hidden, grad_sel, preferred_element_type=jnp.float32)
    w_out_grad = dp_total(w_out_part)

    hid_grad = jnp.einsum("rkto,rkio->tri", grad_sel, w_out, preferred_element_type=jnp.float32)
    pre_grad = (hid_grad * gelu_slope(preact)).astype(jnp.bfloat16)
    in_terms = jnp.einsum("tro,rkio->trki", pre_grad, w_in, preferred_element_type=jnp.float32)
    in_send = chip_sums(in_terms, in_flat)
    got = lax.all_to_all(jnp.stack([out_send, in_send], axis=1), "chip", split_axis=0, concat_axis=0, tiled=True)
    outputs = finish(got[:, 0])
    in_grad = finish(got[:, 1])
    w_in_part = jnp.einsum("rkti,tro->rkio", in_sel, pre_grad, preferred_element_type=jnp.float32)
    w_in_grad = dp_total(w_in_part)
    return (outputs, in_grad, w_in_grad, w_out_grad)


def solution(mesh):
    n_dp, n_mp = mesh.shape["dp"], mesh.shape["mp"]
    pair = 2 if n_mp % 2 == 0 else 1
    split = Mesh(mesh.devices.reshape(n_dp, n_mp // pair, pair), ("dp", "chip", "core"))
    cols = ("chip", "core")
    return jax.shard_map(
        per_device,
        mesh=split,
        in_specs=(
            P("dp", cols),
            P("dp", cols),
            P(cols, None, None, None),
            P(cols, None),
            P(cols, None, None, None),
            P(cols, None),
        ),
        out_specs=(
            P("dp", cols),
            P("dp", cols),
            P(cols, None, None, None),
            P(cols, None, None, None),
        ),
        check_vma=False,
    )
```

```python
import jax
import jax.numpy as jnp
from jax import lax
from jax.sharding import Mesh, PartitionSpec as P

root_half = 0.7071067811865476
inv_root_two_pi = 0.3989422804014327


def gelu_value(preact):
    return 0.5 * preact * (1.0 + jax.scipy.special.erf(preact * root_half))


def gelu_slope(preact):
    return (
        0.5 * (1.0 + jax.scipy.special.erf(preact * root_half))
        + preact * jnp.exp(-0.5 * preact * preact) * inv_root_two_pi
    )


def swap_core(x):
    return lax.ppermute(x, "core", perm=[(0, 1), (1, 0)])


def chip_orders(chips):
    if chips & (chips - 1) or chips < 2:
        return None, None
    steps = []
    step = chips // 2
    while step >= 1:
        steps.append(step)
        step //= 2
    return steps, steps[:1] + steps[1:][::-1]


def gather_chips(x, chips, order):
    if order is None:
        return lax.all_gather(x, "chip", axis=0, tiled=False)
    me = lax.axis_index("chip")
    held = x[None]
    for step in order:
        got = lax.ppermute(held, "chip", perm=[(i, i ^ step) for i in range(chips)])
        upper = (me // step) % 2 == 1
        held = jnp.where(upper, jnp.concatenate([got, held], axis=0), jnp.concatenate([held, got], axis=0))
    return held


def chip_slot(chip, order):
    if order is None:
        return chip
    slot = jnp.zeros_like(chip)
    for k, step in enumerate(order):
        slot = slot + ((chip // step) % 2) * (1 << k)
    return slot


def reduce_chips(buf, chips, order):
    if order is None:
        got = lax.all_to_all(buf.astype(jnp.bfloat16), "chip", split_axis=0, concat_axis=0, tiled=True)
        return got.astype(jnp.float32).sum(axis=0)
    me = lax.axis_index("chip")
    nbits = chips.bit_length() - 1
    rest = buf.shape[1:]
    buf = buf.reshape((2,) * nbits + rest)
    bits = list(range(nbits - 1, -1, -1))
    for step in order:
        bit = step.bit_length() - 1
        axis = bits.index(bit)
        mine = (me // step) % 2
        keep = lax.dynamic_index_in_dim(buf, mine, axis=axis, keepdims=False)
        give = lax.dynamic_index_in_dim(buf, 1 - mine, axis=axis, keepdims=False)
        got = lax.ppermute(give.astype(jnp.bfloat16), "chip", perm=[(i, i ^ step) for i in range(chips)])
        buf = keep + got.astype(jnp.float32)
        bits.pop(axis)
    return buf


def per_device(inputs, out_grad, w_in, in_blocks, w_out, out_blocks):
    tok_rows = inputs.shape[0]
    own_cols = inputs.shape[1]
    hid_rows = w_in.shape[0]
    per_row = w_in.shape[1]
    block_size = w_in.shape[2]
    pair_count = hid_rows * per_row
    chips = lax.axis_size("chip")
    pair = lax.axis_size("core")
    own_blocks = own_cols // block_size
    col_count = chips * pair * own_blocks
    core = lax.axis_index("core")

    order_in, order_grad = chip_orders(chips)

    def gather(x, order):
        x = x.reshape(tok_rows, own_blocks, block_size).transpose(1, 0, 2)
        mine = gather_chips(x, chips, order)
        return jnp.stack([mine, swap_core(mine)], axis=0)

    def select(sets, flat, order):
        owner = flat // own_blocks
        sub = flat % own_blocks
        side = (owner % pair != core).astype(jnp.int32)
        sel = sets[side, chip_slot(owner // pair, order), sub]
        return sel.reshape(hid_rows, per_row, tok_rows, block_size)

    in_flat = in_blocks.reshape(pair_count)
    out_flat = out_blocks.reshape(pair_count)
    in_sel = select(gather(inputs, order_in), in_flat, order_in)
    grad_sel = select(gather(out_grad, order_grad), out_flat, order_grad)

    def dp_total(part):
        part = part.astype(jnp.bfloat16)
        if lax.axis_size("dp") == 2:
            got = lax.ppermute(part, "dp", perm=[(0, 1), (1, 0)])
            return (part.astype(jnp.float32) + got.astype(jnp.float32)).astype(jnp.bfloat16)
        return lax.psum(part, "dp")

    columns = jnp.arange(col_count, dtype=jnp.int32)

    def chip_sums(terms, flat):
        terms = terms.reshape(tok_rows, pair_count, block_size)
        hi = terms.astype(jnp.bfloat16)
        lo = (terms - hi.astype(jnp.float32)).astype(jnp.bfloat16)
        onehot = (flat[:, None] == columns[None, :]).astype(jnp.bfloat16)
        parts = jnp.concatenate([hi, lo], axis=1)
        picks = jnp.concatenate([onehot, onehot], axis=0)
        local = jnp.einsum("tpo,pc->cto", parts, picks, preferred_element_type=jnp.float32)
        local = local.reshape(chips, pair, own_blocks, tok_rows, block_size)
        keep = lax.dynamic_index_in_dim(local, core, axis=1, keepdims=False)
        give = lax.dynamic_index_in_dim(local, 1 - core, axis=1, keepdims=False)
        return keep + swap_core(give)

    def finish(total):
        return total.transpose(1, 0, 2).reshape(tok_rows, own_cols).astype(jnp.bfloat16)

    preact = jnp.einsum("rkti,rkio->tro", in_sel, w_in, preferred_element_type=jnp.float32)
    hidden = gelu_value(preact).astype(jnp.bfloat16)
    out_terms = jnp.einsum("tri,rkio->trko", hidden, w_out, preferred_element_type=jnp.float32)
    out_send = chip_sums(out_terms, out_flat)

    w_out_part = jnp.einsum("tri,rkto->rkio", hidden, grad_sel, preferred_element_type=jnp.float32)
    w_out_grad = dp_total(w_out_part)

    hid_grad = jnp.einsum("rkto,rkio->tri", grad_sel, w_out, preferred_element_type=jnp.float32)
    pre_grad = (hid_grad * gelu_slope(preact)).astype(jnp.bfloat16)
    in_terms = jnp.einsum("tro,rkio->trki", pre_grad, w_in, preferred_element_type=jnp.float32)
    in_send = chip_sums(in_terms, in_flat)
    outputs = finish(reduce_chips(out_send, chips, order_in[::-1] if order_in else None))
    in_grad = finish(reduce_chips(in_send, chips, order_grad[::-1] if order_grad else None))
    w_in_part = jnp.einsum("rkti,tro->rkio", in_sel, pre_grad, preferred_element_type=jnp.float32)
    w_in_grad = dp_total(w_in_part)
    return (outputs, in_grad, w_in_grad, w_out_grad)


def solution(mesh):
    n_dp, n_mp = mesh.shape["dp"], mesh.shape["mp"]
    pair = 2 if n_mp % 2 == 0 else 1
    split = Mesh(mesh.devices.reshape(n_dp, n_mp // pair, pair), ("dp", "chip", "core"))
    cols = ("chip", "core")
    return jax.shard_map(
        per_device,
        mesh=split,
        in_specs=(
            P("dp", cols),
            P("dp", cols),
            P(cols, None, None, None),
            P(cols, None),
            P(cols, None, None, None),
            P(cols, None),
        ),
        out_specs=(
            P("dp", cols),
            P("dp", cols),
            P(cols, None, None, None),
            P(cols, None, None, None),
        ),
        check_vma=False,
    )
```

```python
import jax
import jax.numpy as jnp
from jax import lax
from jax.sharding import Mesh, PartitionSpec as P

root_half = 0.7071067811865476
inv_root_two_pi = 0.3989422804014327


def gelu_value(preact):
    return 0.5 * preact * (1.0 + jax.scipy.special.erf(preact * root_half))


def gelu_slope(preact):
    return (
        0.5 * (1.0 + jax.scipy.special.erf(preact * root_half))
        + preact * jnp.exp(-0.5 * preact * preact) * inv_root_two_pi
    )


def swap_core(x):
    return lax.ppermute(x, "core", perm=[(0, 1), (1, 0)])


def chip_orders(chips):
    if chips & (chips - 1) or chips < 2:
        return None, None
    steps = []
    step = chips // 2
    while step >= 1:
        steps.append(step)
        step //= 2
    return steps, steps[:1] + steps[1:][::-1]


def gather_chips(x, chips, order):
    if order is None:
        return lax.all_gather(x, "chip", axis=0, tiled=False)
    me = lax.axis_index("chip")
    held = x[None]
    for step in order:
        got = lax.ppermute(held, "chip", perm=[(i, i ^ step) for i in range(chips)])
        upper = (me // step) % 2 == 1
        held = jnp.where(upper, jnp.concatenate([got, held], axis=0), jnp.concatenate([held, got], axis=0))
    return held


def chip_slot(chip, order):
    if order is None:
        return chip
    slot = jnp.zeros_like(chip)
    for k, step in enumerate(order):
        slot = slot + ((chip // step) % 2) * (1 << k)
    return slot


def per_device(inputs, out_grad, w_in, in_blocks, w_out, out_blocks):
    tok_rows = inputs.shape[0]
    own_cols = inputs.shape[1]
    hid_rows = w_in.shape[0]
    per_row = w_in.shape[1]
    block_size = w_in.shape[2]
    pair_count = hid_rows * per_row
    chips = lax.axis_size("chip")
    pair = lax.axis_size("core")
    own_blocks = own_cols // block_size
    col_count = chips * pair * own_blocks
    core = lax.axis_index("core")

    order_in, order_grad = chip_orders(chips)

    def gather(x, order):
        x = x.reshape(tok_rows, own_blocks, block_size).transpose(1, 0, 2)
        mine = gather_chips(x, chips, order)
        return jnp.stack([mine, swap_core(mine)], axis=0)

    def select(sets, flat, order):
        owner = flat // own_blocks
        sub = flat % own_blocks
        side = (owner % pair != core).astype(jnp.int32)
        sel = sets[side, chip_slot(owner // pair, order), sub]
        return sel.reshape(hid_rows, per_row, tok_rows, block_size)

    in_flat = in_blocks.reshape(pair_count)
    out_flat = out_blocks.reshape(pair_count)
    in_sel = select(gather(inputs, order_in), in_flat, order_in)
    grad_sel = select(gather(out_grad, order_grad), out_flat, order_grad)

    def dp_total(part):
        part = part.astype(jnp.bfloat16)
        if lax.axis_size("dp") == 2:
            got = lax.ppermute(part, "dp", perm=[(0, 1), (1, 0)])
            return (part.astype(jnp.float32) + got.astype(jnp.float32)).astype(jnp.bfloat16)
        return lax.psum(part, "dp")

    columns = jnp.arange(col_count, dtype=jnp.int32)

    def chip_sums(terms, flat):
        terms = terms.reshape(tok_rows, pair_count, block_size)
        onehot = (flat[:, None] == columns[None, :]).astype(jnp.bfloat16)
        local = jnp.einsum("tpo,pc->cto", terms.astype(jnp.bfloat16), onehot, preferred_element_type=jnp.float32)
        local = local.reshape(chips, pair, own_blocks, tok_rows, block_size)
        keep = lax.dynamic_index_in_dim(local, core, axis=1, keepdims=False)
        give = lax.dynamic_index_in_dim(local, 1 - core, axis=1, keepdims=False)
        return (keep + swap_core(give)).astype(jnp.bfloat16)

    def finish(got):
        total = got.astype(jnp.float32).sum(axis=0)
        return total.transpose(1, 0, 2).reshape(tok_rows, own_cols).astype(jnp.bfloat16)

    preact = jnp.einsum("rkti,rkio->tro", in_sel, w_in, preferred_element_type=jnp.float32)
    hidden = gelu_value(preact).astype(jnp.bfloat16)
    out_terms = jnp.einsum("tri,rkio->trko", hidden, w_out, preferred_element_type=jnp.float32)
    out_send = chip_sums(out_terms, out_flat)

    w_out_part = jnp.einsum("tri,rkto->rkio", hidden, grad_sel, preferred_element_type=jnp.float32)
    w_out_grad = dp_total(w_out_part)

    hid_grad = jnp.einsum("rkto,rkio->tri", grad_sel, w_out, preferred_element_type=jnp.float32)
    pre_grad = (hid_grad * gelu_slope(preact)).astype(jnp.bfloat16)
    in_terms = jnp.einsum("tro,rkio->trki", pre_grad, w_in, preferred_element_type=jnp.float32)
    in_send = chip_sums(in_terms, in_flat)
    got = lax.all_to_all(jnp.stack([out_send, in_send], axis=1), "chip", split_axis=0, concat_axis=0, tiled=True)
    outputs = finish(got[:, 0])
    in_grad = finish(got[:, 1])
    w_in_part = jnp.einsum("rkti,tro->rkio", in_sel, pre_grad, preferred_element_type=jnp.float32)
    w_in_grad = dp_total(w_in_part)
    return (outputs, in_grad, w_in_grad, w_out_grad)


def solution(mesh):
    n_dp, n_mp = mesh.shape["dp"], mesh.shape["mp"]
    pair = 2 if n_mp % 2 == 0 else 1
    split = Mesh(mesh.devices.reshape(n_dp, n_mp // pair, pair), ("dp", "chip", "core"))
    cols = ("chip", "core")
    return jax.shard_map(
        per_device,
        mesh=split,
        in_specs=(
            P("dp", cols),
            P("dp", cols),
            P(cols, None, None, None),
            P(cols, None),
            P(cols, None, None, None),
            P(cols, None),
        ),
        out_specs=(
            P("dp", cols),
            P("dp", cols),
            P(cols, None, None, None),
            P(cols, None, None, None),
        ),
        check_vma=False,
    )
```

```python
import jax
import jax.numpy as jnp
from jax import lax
from jax.sharding import Mesh, PartitionSpec as P

root_half = 0.7071067811865476
inv_root_two_pi = 0.3989422804014327


def gelu_value(preact):
    return 0.5 * preact * (1.0 + jax.scipy.special.erf(preact * root_half))


def gelu_slope(preact):
    return (
        0.5 * (1.0 + jax.scipy.special.erf(preact * root_half))
        + preact * jnp.exp(-0.5 * preact * preact) * inv_root_two_pi
    )


def swap_core(x):
    return lax.ppermute(x, "core", perm=[(0, 1), (1, 0)])


def chip_orders(chips):
    if chips & (chips - 1) or chips < 2:
        return None, None
    steps = []
    step = chips // 2
    while step >= 1:
        steps.append(step)
        step //= 2
    return steps, steps[:1] + steps[1:][::-1]


def gather_chips(x, chips, order):
    if order is None:
        return lax.all_gather(x, "chip", axis=0, tiled=False)
    me = lax.axis_index("chip")
    held = x[None]
    for step in order:
        got = lax.ppermute(held, "chip", perm=[(i, i ^ step) for i in range(chips)])
        upper = (me // step) % 2 == 1
        held = jnp.where(upper, jnp.concatenate([got, held], axis=0), jnp.concatenate([held, got], axis=0))
    return held


def chip_slot(chip, order):
    if order is None:
        return chip
    slot = jnp.zeros_like(chip)
    for k, step in enumerate(order):
        slot = slot + ((chip // step) % 2) * (1 << k)
    return slot


def per_device(inputs, out_grad, w_in, in_blocks, w_out, out_blocks):
    tok_rows = inputs.shape[0]
    own_cols = inputs.shape[1]
    hid_rows = w_in.shape[0]
    per_row = w_in.shape[1]
    block_size = w_in.shape[2]
    pair_count = hid_rows * per_row
    chips = lax.axis_size("chip")
    pair = lax.axis_size("core")
    own_blocks = own_cols // block_size
    col_count = chips * pair * own_blocks
    core = lax.axis_index("core")

    order_in, order_grad = chip_orders(chips)

    def gather(x, order):
        x = x.reshape(tok_rows, own_blocks, block_size).transpose(1, 0, 2)
        mine = gather_chips(x, chips, order)
        return jnp.stack([mine, swap_core(mine)], axis=0)

    def select(sets, flat, order):
        owner = flat // own_blocks
        sub = flat % own_blocks
        side = (owner % pair != core).astype(jnp.int32)
        sel = sets[side, chip_slot(owner // pair, order), sub]
        return sel.reshape(hid_rows, per_row, tok_rows, block_size)

    in_flat = in_blocks.reshape(pair_count)
    out_flat = out_blocks.reshape(pair_count)
    in_sel = select(gather(inputs, order_in), in_flat, order_in)
    grad_sel = select(gather(out_grad, order_grad), out_flat, order_grad)

    def dp_total(part):
        part = part.astype(jnp.bfloat16)
        if lax.axis_size("dp") == 2:
            got = lax.ppermute(part, "dp", perm=[(0, 1), (1, 0)])
            return (part.astype(jnp.float32) + got.astype(jnp.float32)).astype(jnp.bfloat16)
        return lax.psum(part, "dp")

    columns = jnp.arange(col_count, dtype=jnp.int32)

    def chip_sums(terms, flat):
        terms = terms.reshape(tok_rows, pair_count, block_size)
        onehot = (flat[:, None] == columns[None, :]).astype(jnp.bfloat16)
        local = jnp.einsum("tpo,pc->cto", terms.astype(jnp.bfloat16), onehot, preferred_element_type=jnp.float32)
        local = local.reshape(chips, pair, own_blocks, tok_rows, block_size)
        keep = lax.dynamic_index_in_dim(local, core, axis=1, keepdims=False)
        give = lax.dynamic_index_in_dim(local, 1 - core, axis=1, keepdims=False)
        return (keep + swap_core(give.astype(jnp.bfloat16)).astype(jnp.float32)).astype(jnp.bfloat16)

    def finish(got):
        total = got.astype(jnp.float32).sum(axis=0)
        return total.transpose(1, 0, 2).reshape(tok_rows, own_cols).astype(jnp.bfloat16)

    preact = jnp.einsum("rkti,rkio->tro", in_sel, w_in, preferred_element_type=jnp.float32)
    hidden = gelu_value(preact).astype(jnp.bfloat16)
    out_terms = jnp.einsum("tri,rkio->trko", hidden, w_out, preferred_element_type=jnp.float32)
    out_send = chip_sums(out_terms, out_flat)

    w_out_part = jnp.einsum("tri,rkto->rkio", hidden, grad_sel, preferred_element_type=jnp.float32)
    w_out_grad = dp_total(w_out_part)

    hid_grad = jnp.einsum("rkto,rkio->tri", grad_sel, w_out, preferred_element_type=jnp.float32)
    pre_grad = (hid_grad * gelu_slope(preact)).astype(jnp.bfloat16)
    in_terms = jnp.einsum("tro,rkio->trki", pre_grad, w_in, preferred_element_type=jnp.float32)
    in_send = chip_sums(in_terms, in_flat)
    got = lax.all_to_all(jnp.stack([out_send, in_send], axis=1), "chip", split_axis=0, concat_axis=0, tiled=True)
    outputs = finish(got[:, 0])
    in_grad = finish(got[:, 1])
    w_in_part = jnp.einsum("rkti,tro->rkio", in_sel, pre_grad, preferred_element_type=jnp.float32)
    w_in_grad = dp_total(w_in_part)
    return (outputs, in_grad, w_in_grad, w_out_grad)


def solution(mesh):
    n_dp, n_mp = mesh.shape["dp"], mesh.shape["mp"]
    pair = 2 if n_mp % 2 == 0 else 1
    split = Mesh(mesh.devices.reshape(n_dp, n_mp // pair, pair), ("dp", "chip", "core"))
    cols = ("chip", "core")
    return jax.shard_map(
        per_device,
        mesh=split,
        in_specs=(
            P("dp", cols),
            P("dp", cols),
            P(cols, None, None, None),
            P(cols, None),
            P(cols, None, None, None),
            P(cols, None),
        ),
        out_specs=(
            P("dp", cols),
            P("dp", cols),
            P(cols, None, None, None),
            P(cols, None, None, None),
        ),
        check_vma=False,
    )
```

```python
import jax
import jax.numpy as jnp
from jax import lax
from jax.sharding import Mesh, PartitionSpec as P

root_half = 0.7071067811865476
inv_root_two_pi = 0.3989422804014327


def gelu_value(preact):
    return 0.5 * preact * (1.0 + jax.scipy.special.erf(preact * root_half))


def gelu_slope(preact):
    return (
        0.5 * (1.0 + jax.scipy.special.erf(preact * root_half))
        + preact * jnp.exp(-0.5 * preact * preact) * inv_root_two_pi
    )


def swap_core(x):
    return lax.ppermute(x, "core", perm=[(0, 1), (1, 0)])


def chip_orders(chips):
    if chips & (chips - 1) or chips < 2:
        return None, None
    steps = []
    step = chips // 2
    while step >= 1:
        steps.append(step)
        step //= 2
    return steps, steps[:1] + steps[1:][::-1]


def gather_chips(x, chips, order):
    if order is None:
        return lax.all_gather(x, "chip", axis=0, tiled=False)
    held = x[None]
    for step in order:
        got = lax.ppermute(held, "chip", perm=[(i, i ^ step) for i in range(chips)])
        held = jnp.concatenate([held, got], axis=0)
    return held


def chip_slot(chip, order):
    if order is None:
        return chip
    me = lax.axis_index("chip")
    slot = jnp.zeros_like(chip)
    for k, step in enumerate(order):
        slot = slot + ((chip // step) % 2 != (me // step) % 2).astype(chip.dtype) * (1 << k)
    return slot


def per_device(inputs, out_grad, w_in, in_blocks, w_out, out_blocks):
    tok_rows = inputs.shape[0]
    own_cols = inputs.shape[1]
    hid_rows = w_in.shape[0]
    per_row = w_in.shape[1]
    block_size = w_in.shape[2]
    pair_count = hid_rows * per_row
    chips = lax.axis_size("chip")
    pair = lax.axis_size("core")
    own_blocks = own_cols // block_size
    col_count = chips * pair * own_blocks
    core = lax.axis_index("core")

    order_in, order_grad = chip_orders(chips)

    def gather(x, order):
        x = x.reshape(tok_rows, own_blocks, block_size).transpose(1, 0, 2)
        mine = gather_chips(x, chips, order)
        return jnp.stack([mine, swap_core(mine)], axis=0)

    def select(sets, flat, order):
        owner = flat // own_blocks
        sub = flat % own_blocks
        side = (owner % pair != core).astype(jnp.int32)
        sel = sets[side, chip_slot(owner // pair, order), sub]
        return sel.reshape(hid_rows, per_row, tok_rows, block_size)

    in_flat = in_blocks.reshape(pair_count)
    out_flat = out_blocks.reshape(pair_count)
    in_sel = select(gather(inputs, order_in), in_flat, order_in)
    grad_sel = select(gather(out_grad, order_grad), out_flat, order_grad)

    def dp_total(part):
        part = part.astype(jnp.bfloat16)
        if lax.axis_size("dp") == 2:
            got = lax.ppermute(part, "dp", perm=[(0, 1), (1, 0)])
            return (part.astype(jnp.float32) + got.astype(jnp.float32)).astype(jnp.bfloat16)
        return lax.psum(part, "dp")

    columns = jnp.arange(col_count, dtype=jnp.int32)

    def chip_sums(terms, flat):
        terms = terms.reshape(tok_rows, pair_count, block_size)
        onehot = (flat[:, None] == columns[None, :]).astype(jnp.bfloat16)
        local = jnp.einsum("tpo,pc->cto", terms.astype(jnp.bfloat16), onehot, preferred_element_type=jnp.float32)
        local = local.reshape(chips, pair, own_blocks, tok_rows, block_size)
        keep = lax.dynamic_index_in_dim(local, core, axis=1, keepdims=False)
        give = lax.dynamic_index_in_dim(local, 1 - core, axis=1, keepdims=False)
        return (keep + swap_core(give)).astype(jnp.bfloat16)

    def finish(got):
        total = got.astype(jnp.float32).sum(axis=0)
        return total.transpose(1, 0, 2).reshape(tok_rows, own_cols).astype(jnp.bfloat16)

    preact = jnp.einsum("rkti,rkio->tro", in_sel, w_in, preferred_element_type=jnp.float32)
    hidden = gelu_value(preact).astype(jnp.bfloat16)
    out_terms = jnp.einsum("tri,rkio->trko", hidden, w_out, preferred_element_type=jnp.float32)
    out_send = chip_sums(out_terms, out_flat)

    w_out_part = jnp.einsum("tri,rkto->rkio", hidden, grad_sel, preferred_element_type=jnp.float32)
    w_out_grad = dp_total(w_out_part)

    hid_grad = jnp.einsum("rkto,rkio->tri", grad_sel, w_out, preferred_element_type=jnp.float32)
    pre_grad = (hid_grad * gelu_slope(preact)).astype(jnp.bfloat16)
    in_terms = jnp.einsum("tro,rkio->trki", pre_grad, w_in, preferred_element_type=jnp.float32)
    in_send = chip_sums(in_terms, in_flat)
    got = lax.all_to_all(jnp.stack([out_send, in_send], axis=1), "chip", split_axis=0, concat_axis=0, tiled=True)
    outputs = finish(got[:, 0])
    in_grad = finish(got[:, 1])
    w_in_part = jnp.einsum("rkti,tro->rkio", in_sel, pre_grad, preferred_element_type=jnp.float32)
    w_in_grad = dp_total(w_in_part)
    return (outputs, in_grad, w_in_grad, w_out_grad)


def solution(mesh):
    n_dp, n_mp = mesh.shape["dp"], mesh.shape["mp"]
    pair = 2 if n_mp % 2 == 0 else 1
    split = Mesh(mesh.devices.reshape(n_dp, n_mp // pair, pair), ("dp", "chip", "core"))
    cols = ("chip", "core")
    return jax.shard_map(
        per_device,
        mesh=split,
        in_specs=(
            P("dp", cols),
            P("dp", cols),
            P(cols, None, None, None),
            P(cols, None),
            P(cols, None, None, None),
            P(cols, None),
        ),
        out_specs=(
            P("dp", cols),
            P("dp", cols),
            P(cols, None, None, None),
            P(cols, None, None, None),
        ),
        check_vma=False,
    )
```

```python
import jax
import jax.numpy as jnp
from jax import lax
from jax.sharding import Mesh, PartitionSpec as P

root_half = 0.7071067811865476
inv_root_two_pi = 0.3989422804014327


def gelu_value(preact):
    return 0.5 * preact * (1.0 + jax.scipy.special.erf(preact * root_half))


def gelu_slope(preact):
    return (
        0.5 * (1.0 + jax.scipy.special.erf(preact * root_half))
        + preact * jnp.exp(-0.5 * preact * preact) * inv_root_two_pi
    )


def swap_core(x):
    return lax.ppermute(x, "core", perm=[(0, 1), (1, 0)])


def chip_orders(chips):
    if chips & (chips - 1) or chips < 2:
        return None, None
    steps = []
    step = chips // 2
    while step >= 1:
        steps.append(step)
        step //= 2
    return steps, steps[:1] + steps[1:][::-1]


def gather_chips(x, chips, order):
    if order is None:
        return lax.all_gather(x, "chip", axis=0, tiled=False)
    me = lax.axis_index("chip")
    held = x[None]
    for step in order:
        got = lax.ppermute(held, "chip", perm=[(i, i ^ step) for i in range(chips)])
        upper = (me // step) % 2 == 1
        held = jnp.where(upper, jnp.concatenate([got, held], axis=0), jnp.concatenate([held, got], axis=0))
    return held


def chip_slot(chip, order):
    if order is None:
        return chip
    slot = jnp.zeros_like(chip)
    for k, step in enumerate(order):
        slot = slot + ((chip // step) % 2) * (1 << k)
    return slot


def per_device(inputs, out_grad, w_in, in_blocks, w_out, out_blocks):
    tok_rows = inputs.shape[0]
    own_cols = inputs.shape[1]
    hid_rows = w_in.shape[0]
    per_row = w_in.shape[1]
    block_size = w_in.shape[2]
    pair_count = hid_rows * per_row
    chips = lax.axis_size("chip")
    pair = lax.axis_size("core")
    own_blocks = own_cols // block_size
    col_count = chips * pair * own_blocks
    core = lax.axis_index("core")

    order_grad, order_in = chip_orders(chips)

    def gather(x, order):
        x = x.reshape(tok_rows, own_blocks, block_size).transpose(1, 0, 2)
        mine = gather_chips(x, chips, order)
        return jnp.stack([mine, swap_core(mine)], axis=0)

    def select(sets, flat, order):
        owner = flat // own_blocks
        sub = flat % own_blocks
        side = (owner % pair != core).astype(jnp.int32)
        sel = sets[side, chip_slot(owner // pair, order), sub]
        return sel.reshape(hid_rows, per_row, tok_rows, block_size)

    in_flat = in_blocks.reshape(pair_count)
    out_flat = out_blocks.reshape(pair_count)
    in_sel = select(gather(inputs, order_in), in_flat, order_in)
    grad_sel = select(gather(out_grad, order_grad), out_flat, order_grad)

    def dp_total(part):
        part = part.astype(jnp.bfloat16)
        if lax.axis_size("dp") == 2:
            got = lax.ppermute(part, "dp", perm=[(0, 1), (1, 0)])
            return (part.astype(jnp.float32) + got.astype(jnp.float32)).astype(jnp.bfloat16)
        return lax.psum(part, "dp")

    columns = jnp.arange(col_count, dtype=jnp.int32)

    def chip_sums(terms, flat):
        terms = terms.reshape(tok_rows, pair_count, block_size)
        onehot = (flat[:, None] == columns[None, :]).astype(jnp.bfloat16)
        local = jnp.einsum("tpo,pc->cto", terms.astype(jnp.bfloat16), onehot, preferred_element_type=jnp.float32)
        local = local.reshape(chips, pair, own_blocks, tok_rows, block_size)
        keep = lax.dynamic_index_in_dim(local, core, axis=1, keepdims=False)
        give = lax.dynamic_index_in_dim(local, 1 - core, axis=1, keepdims=False)
        return (keep + swap_core(give)).astype(jnp.bfloat16)

    def finish(got):
        total = got.astype(jnp.float32).sum(axis=0)
        return total.transpose(1, 0, 2).reshape(tok_rows, own_cols).astype(jnp.bfloat16)

    preact = jnp.einsum("rkti,rkio->tro", in_sel, w_in, preferred_element_type=jnp.float32)
    hidden = gelu_value(preact).astype(jnp.bfloat16)
    out_terms = jnp.einsum("tri,rkio->trko", hidden, w_out, preferred_element_type=jnp.float32)
    out_send = chip_sums(out_terms, out_flat)

    w_out_part = jnp.einsum("tri,rkto->rkio", hidden, grad_sel, preferred_element_type=jnp.float32)
    w_out_grad = dp_total(w_out_part)

    hid_grad = jnp.einsum("rkto,rkio->tri", grad_sel, w_out, preferred_element_type=jnp.float32)
    pre_grad = (hid_grad * gelu_slope(preact)).astype(jnp.bfloat16)
    in_terms = jnp.einsum("tro,rkio->trki", pre_grad, w_in, preferred_element_type=jnp.float32)
    in_send = chip_sums(in_terms, in_flat)
    got = lax.all_to_all(jnp.stack([out_send, in_send], axis=1), "chip", split_axis=0, concat_axis=0, tiled=True)
    outputs = finish(got[:, 0])
    in_grad = finish(got[:, 1])
    w_in_part = jnp.einsum("rkti,tro->rkio", in_sel, pre_grad, preferred_element_type=jnp.float32)
    w_in_grad = dp_total(w_in_part)
    return (outputs, in_grad, w_in_grad, w_out_grad)


def solution(mesh):
    n_dp, n_mp = mesh.shape["dp"], mesh.shape["mp"]
    pair = 2 if n_mp % 2 == 0 else 1
    split = Mesh(mesh.devices.reshape(n_dp, n_mp // pair, pair), ("dp", "chip", "core"))
    cols = ("chip", "core")
    return jax.shard_map(
        per_device,
        mesh=split,
        in_specs=(
            P("dp", cols),
            P("dp", cols),
            P(cols, None, None, None),
            P(cols, None),
            P(cols, None, None, None),
            P(cols, None),
        ),
        out_specs=(
            P("dp", cols),
            P("dp", cols),
            P(cols, None, None, None),
            P(cols, None, None, None),
        ),
        check_vma=False,
    )
```

```python
import jax
import jax.numpy as jnp
from jax import lax
from jax.sharding import Mesh, PartitionSpec as P

root_half = 0.7071067811865476
inv_root_two_pi = 0.3989422804014327


def gelu_value(preact):
    return 0.5 * preact * (1.0 + jax.scipy.special.erf(preact * root_half))


def gelu_slope(preact):
    return (
        0.5 * (1.0 + jax.scipy.special.erf(preact * root_half))
        + preact * jnp.exp(-0.5 * preact * preact) * inv_root_two_pi
    )


def swap_core(x):
    return lax.ppermute(x, "core", perm=[(0, 1), (1, 0)])


def chip_orders(chips):
    if chips & (chips - 1) or chips < 2:
        return None, None
    steps = []
    step = chips // 2
    while step >= 1:
        steps.append(step)
        step //= 2
    return steps, steps[:1] + steps[1:][::-1]


def gather_chips(x, chips, order):
    if order is None:
        return lax.all_gather(x, "chip", axis=0, tiled=False)
    me = lax.axis_index("chip")
    held = x[None]
    for step in order:
        got = lax.ppermute(held, "chip", perm=[(i, i ^ step) for i in range(chips)])
        upper = (me // step) % 2 == 1
        held = jnp.where(upper, jnp.concatenate([got, held], axis=0), jnp.concatenate([held, got], axis=0))
    return held


def chip_slot(chip, order):
    if order is None:
        return chip
    slot = jnp.zeros_like(chip)
    for k, step in enumerate(order):
        slot = slot + ((chip // step) % 2) * (1 << k)
    return slot


def per_device(inputs, out_grad, w_in, in_blocks, w_out, out_blocks):
    tok_rows = inputs.shape[0]
    own_cols = inputs.shape[1]
    hid_rows = w_in.shape[0]
    per_row = w_in.shape[1]
    block_size = w_in.shape[2]
    pair_count = hid_rows * per_row
    chips = lax.axis_size("chip")
    pair = lax.axis_size("core")
    own_blocks = own_cols // block_size
    col_count = chips * pair * own_blocks
    core = lax.axis_index("core")

    order_grad, order_in = chip_orders(chips)

    def gather(x, order):
        x = x.reshape(tok_rows, own_blocks, block_size).transpose(1, 0, 2)
        mine = gather_chips(x, chips, order)
        return jnp.stack([mine, swap_core(mine)], axis=0)

    def select(sets, flat, order):
        owner = flat // own_blocks
        sub = flat % own_blocks
        side = (owner % pair != core).astype(jnp.int32)
        sel = sets[side, chip_slot(owner // pair, order), sub]
        return sel.reshape(hid_rows, per_row, tok_rows, block_size)

    in_flat = in_blocks.reshape(pair_count)
    out_flat = out_blocks.reshape(pair_count)
    in_sel = select(gather(inputs, order_in), in_flat, order_in)
    grad_sel = select(gather(out_grad, order_grad), out_flat, order_grad)

    def dp_total(part):
        part = part.astype(jnp.bfloat16)
        if lax.axis_size("dp") == 2:
            got = lax.ppermute(part, "dp", perm=[(0, 1), (1, 0)])
            return (part.astype(jnp.float32) + got.astype(jnp.float32)).astype(jnp.bfloat16)
        return lax.psum(part, "dp")

    columns = jnp.arange(col_count, dtype=jnp.int32)

    def chip_sums(terms, flat):
        terms = terms.reshape(tok_rows, pair_count, block_size)
        onehot = (flat[:, None] == columns[None, :]).astype(jnp.bfloat16)
        local = jnp.einsum("tpo,pc->cto", terms.astype(jnp.bfloat16), onehot, preferred_element_type=jnp.float32)
        local = local.reshape(chips, pair, own_blocks, tok_rows, block_size)
        keep = lax.dynamic_index_in_dim(local, core, axis=1, keepdims=False)
        give = lax.dynamic_index_in_dim(local, 1 - core, axis=1, keepdims=False)
        return (keep + swap_core(give)).astype(jnp.bfloat16)

    def finish(got):
        total = got.astype(jnp.float32).sum(axis=0)
        return total.transpose(1, 0, 2).reshape(tok_rows, own_cols).astype(jnp.bfloat16)

    preact = jnp.einsum("rkti,rkio->tro", in_sel, w_in, preferred_element_type=jnp.float32)
    hidden = gelu_value(preact).astype(jnp.bfloat16)
    out_terms = jnp.einsum("tri,rkio->trko", hidden, w_out, preferred_element_type=jnp.float32)
    out_send = chip_sums(out_terms, out_flat)

    w_out_part = jnp.einsum("tri,rkto->rkio", hidden, grad_sel, preferred_element_type=jnp.float32)

    hid_grad = jnp.einsum("rkto,rkio->tri", grad_sel, w_out, preferred_element_type=jnp.float32)
    pre_grad = (hid_grad * gelu_slope(preact)).astype(jnp.bfloat16)
    in_terms = jnp.einsum("tro,rkio->trki", pre_grad, w_in, preferred_element_type=jnp.float32)
    in_send = chip_sums(in_terms, in_flat)
    got = lax.all_to_all(jnp.stack([out_send, in_send], axis=1), "chip", split_axis=0, concat_axis=0, tiled=True)
    outputs = finish(got[:, 0])
    in_grad = finish(got[:, 1])
    w_in_part = jnp.einsum("rkti,tro->rkio", in_sel, pre_grad, preferred_element_type=jnp.float32)
    w_both = dp_total(jnp.stack([w_in_part, w_out_part], axis=0))
    w_in_grad, w_out_grad = w_both[0], w_both[1]
    return (outputs, in_grad, w_in_grad, w_out_grad)


def solution(mesh):
    n_dp, n_mp = mesh.shape["dp"], mesh.shape["mp"]
    pair = 2 if n_mp % 2 == 0 else 1
    split = Mesh(mesh.devices.reshape(n_dp, n_mp // pair, pair), ("dp", "chip", "core"))
    cols = ("chip", "core")
    return jax.shard_map(
        per_device,
        mesh=split,
        in_specs=(
            P("dp", cols),
            P("dp", cols),
            P(cols, None, None, None),
            P(cols, None),
            P(cols, None, None, None),
            P(cols, None),
        ),
        out_specs=(
            P("dp", cols),
            P("dp", cols),
            P(cols, None, None, None),
            P(cols, None, None, None),
        ),
        check_vma=False,
    )
```

```python
import jax
import jax.numpy as jnp
from jax import lax
from jax.sharding import Mesh, PartitionSpec as P

root_half = 0.7071067811865476
inv_root_two_pi = 0.3989422804014327


def gelu_value(preact):
    return 0.5 * preact * (1.0 + jax.scipy.special.erf(preact * root_half))


def gelu_slope(preact):
    return (
        0.5 * (1.0 + jax.scipy.special.erf(preact * root_half))
        + preact * jnp.exp(-0.5 * preact * preact) * inv_root_two_pi
    )


def swap_core(x):
    return lax.ppermute(x, "core", perm=[(0, 1), (1, 0)])


def chip_orders(chips):
    if chips & (chips - 1) or chips < 2:
        return None, None
    steps = []
    step = chips // 2
    while step >= 1:
        steps.append(step)
        step //= 2
    return steps, steps[:1] + steps[1:][::-1]


def gather_chips(x, chips, order):
    if order is None:
        return lax.all_gather(x, "chip", axis=0, tiled=False)
    me = lax.axis_index("chip")
    held = x[None]
    for step in order:
        got = lax.ppermute(held, "chip", perm=[(i, i ^ step) for i in range(chips)])
        upper = (me // step) % 2 == 1
        held = jnp.where(upper, jnp.concatenate([got, held], axis=0), jnp.concatenate([held, got], axis=0))
    return held


def chip_slot(chip, order):
    if order is None:
        return chip
    slot = jnp.zeros_like(chip)
    for k, step in enumerate(order):
        slot = slot + ((chip // step) % 2) * (1 << k)
    return slot


def per_device(inputs, out_grad, w_in, in_blocks, w_out, out_blocks):
    tok_rows = inputs.shape[0]
    own_cols = inputs.shape[1]
    hid_rows = w_in.shape[0]
    per_row = w_in.shape[1]
    block_size = w_in.shape[2]
    pair_count = hid_rows * per_row
    chips = lax.axis_size("chip")
    pair = lax.axis_size("core")
    own_blocks = own_cols // block_size
    col_count = chips * pair * own_blocks
    core = lax.axis_index("core")

    order_grad, order_in = chip_orders(chips)

    def gather(x, order):
        x = x.reshape(tok_rows, own_blocks, block_size).transpose(1, 0, 2)
        mine = gather_chips(x, chips, order)
        return jnp.stack([mine, swap_core(mine)], axis=0)

    def select(sets, flat, order):
        owner = flat // own_blocks
        sub = flat % own_blocks
        side = (owner % pair != core).astype(jnp.int32)
        sel = sets[side, chip_slot(owner // pair, order), sub]
        return sel.reshape(hid_rows, per_row, tok_rows, block_size)

    in_flat = in_blocks.reshape(pair_count)
    out_flat = out_blocks.reshape(pair_count)
    in_sel = select(gather(inputs, order_in), in_flat, order_in)
    grad_sel = select(gather(out_grad, order_grad), out_flat, order_grad)

    def dp_total(part):
        part = part.astype(jnp.bfloat16)
        if lax.axis_size("dp") == 2:
            got = lax.ppermute(part, "dp", perm=[(0, 1), (1, 0)])
            return (part.astype(jnp.float32) + got.astype(jnp.float32)).astype(jnp.bfloat16)
        return lax.psum(part, "dp")

    chip_ids = jnp.arange(chips, dtype=jnp.int32)
    sub_ids = jnp.arange(own_blocks, dtype=jnp.int32)

    def chip_sums(terms, flat):
        terms = terms.reshape(tok_rows, pair_count, block_size)
        terms = terms.astype(jnp.bfloat16)

        def half(side):
            cols = (chip_ids[:, None] * pair + side) * own_blocks + sub_ids[None, :]
            onehot = (flat[:, None] == cols.reshape(1, -1)).astype(jnp.bfloat16)
            got = jnp.einsum("tpo,pc->cto", terms, onehot, preferred_element_type=jnp.float32)
            return got.reshape(chips, own_blocks, tok_rows, block_size)

        return (half(core) + swap_core(half(1 - core))).astype(jnp.bfloat16)

    def finish(got):
        total = got.astype(jnp.float32).sum(axis=0)
        return total.transpose(1, 0, 2).reshape(tok_rows, own_cols).astype(jnp.bfloat16)

    preact = jnp.einsum("rkti,rkio->tro", in_sel, w_in, preferred_element_type=jnp.float32)
    hidden = gelu_value(preact).astype(jnp.bfloat16)
    out_terms = jnp.einsum("tri,rkio->trko", hidden, w_out, preferred_element_type=jnp.float32)
    out_send = chip_sums(out_terms, out_flat)

    w_out_part = jnp.einsum("tri,rkto->rkio", hidden, grad_sel, preferred_element_type=jnp.float32)
    w_out_grad = dp_total(w_out_part)

    hid_grad = jnp.einsum("rkto,rkio->tri", grad_sel, w_out, preferred_element_type=jnp.float32)
    pre_grad = (hid_grad * gelu_slope(preact)).astype(jnp.bfloat16)
    in_terms = jnp.einsum("tro,rkio->trki", pre_grad, w_in, preferred_element_type=jnp.float32)
    in_send = chip_sums(in_terms, in_flat)
    got = lax.all_to_all(jnp.stack([out_send, in_send], axis=1), "chip", split_axis=0, concat_axis=0, tiled=True)
    outputs = finish(got[:, 0])
    in_grad = finish(got[:, 1])
    w_in_part = jnp.einsum("rkti,tro->rkio", in_sel, pre_grad, preferred_element_type=jnp.float32)
    w_in_grad = dp_total(w_in_part)
    return (outputs, in_grad, w_in_grad, w_out_grad)


def solution(mesh):
    n_dp, n_mp = mesh.shape["dp"], mesh.shape["mp"]
    pair = 2 if n_mp % 2 == 0 else 1
    split = Mesh(mesh.devices.reshape(n_dp, n_mp // pair, pair), ("dp", "chip", "core"))
    cols = ("chip", "core")
    return jax.shard_map(
        per_device,
        mesh=split,
        in_specs=(
            P("dp", cols),
            P("dp", cols),
            P(cols, None, None, None),
            P(cols, None),
            P(cols, None, None, None),
            P(cols, None),
        ),
        out_specs=(
            P("dp", cols),
            P("dp", cols),
            P(cols, None, None, None),
            P(cols, None, None, None),
        ),
        check_vma=False,
    )
```

```python
import jax
import jax.numpy as jnp
from jax import lax
from jax.sharding import Mesh, PartitionSpec as P

root_half = 0.7071067811865476
inv_root_two_pi = 0.3989422804014327


def gelu_value(preact):
    return 0.5 * preact * (1.0 + jax.scipy.special.erf(preact * root_half))


def gelu_slope(preact):
    return (
        0.5 * (1.0 + jax.scipy.special.erf(preact * root_half))
        + preact * jnp.exp(-0.5 * preact * preact) * inv_root_two_pi
    )


def swap_core(x):
    return lax.ppermute(x, "core", perm=[(0, 1), (1, 0)])


def chip_orders(chips):
    if chips & (chips - 1) or chips < 2:
        return None, None
    steps = []
    step = chips // 2
    while step >= 1:
        steps.append(step)
        step //= 2
    return steps, steps[:1] + steps[1:][::-1]


def gather_chips(x, chips, order):
    if order is None:
        return lax.all_gather(x, "chip", axis=0, tiled=False)
    me = lax.axis_index("chip")
    held = x[None]
    for step in order:
        got = lax.ppermute(held, "chip", perm=[(i, i ^ step) for i in range(chips)])
        upper = (me // step) % 2 == 1
        held = jnp.where(upper, jnp.concatenate([got, held], axis=0), jnp.concatenate([held, got], axis=0))
    return held


def chip_slot(chip, order):
    if order is None:
        return chip
    slot = jnp.zeros_like(chip)
    for k, step in enumerate(order):
        slot = slot + ((chip // step) % 2) * (1 << k)
    return slot


def per_device(inputs, out_grad, w_in, in_blocks, w_out, out_blocks):
    tok_rows = inputs.shape[0]
    own_cols = inputs.shape[1]
    hid_rows = w_in.shape[0]
    per_row = w_in.shape[1]
    block_size = w_in.shape[2]
    pair_count = hid_rows * per_row
    chips = lax.axis_size("chip")
    pair = lax.axis_size("core")
    own_blocks = own_cols // block_size
    col_count = chips * pair * own_blocks
    core = lax.axis_index("core")

    order_grad, order_in = chip_orders(chips)

    def gather(x, order):
        x = x.reshape(tok_rows, own_blocks, block_size).transpose(1, 0, 2)
        mine = gather_chips(x, chips, order)
        return jnp.stack([mine, swap_core(mine)], axis=0)

    def select(sets, flat, order):
        owner = flat // own_blocks
        sub = flat % own_blocks
        side = (owner % pair != core).astype(jnp.int32)
        sel = sets[side, chip_slot(owner // pair, order), sub]
        return sel.reshape(hid_rows, per_row, tok_rows, block_size)

    in_flat = in_blocks.reshape(pair_count)
    out_flat = out_blocks.reshape(pair_count)
    in_sel = select(gather(inputs, order_in), in_flat, order_in)
    grad_sel = select(gather(out_grad, order_grad), out_flat, order_grad)

    def dp_total(part):
        part = part.astype(jnp.bfloat16)
        if lax.axis_size("dp") == 2:
            got = lax.ppermute(part, "dp", perm=[(0, 1), (1, 0)])
            return (part.astype(jnp.float32) + got.astype(jnp.float32)).astype(jnp.bfloat16)
        return lax.psum(part, "dp")

    columns = jnp.arange(col_count, dtype=jnp.int32)

    def chip_sums(terms, flat):
        terms = terms.reshape(tok_rows, pair_count, block_size)
        onehot = (flat[:, None] == columns[None, :]).astype(jnp.bfloat16)
        local = jnp.einsum("tpo,pc->tco", terms.astype(jnp.bfloat16), onehot, preferred_element_type=jnp.float32)
        local = local.reshape(tok_rows, chips, pair, own_blocks, block_size)
        keep = lax.dynamic_index_in_dim(local, core, axis=2, keepdims=False)
        give = lax.dynamic_index_in_dim(local, 1 - core, axis=2, keepdims=False)
        return (keep + swap_core(give)).astype(jnp.bfloat16)

    def finish(got):
        return got.astype(jnp.float32).sum(axis=1).reshape(tok_rows, own_cols).astype(jnp.bfloat16)

    preact = jnp.einsum("rkti,rkio->tro", in_sel, w_in, preferred_element_type=jnp.float32)
    hidden = gelu_value(preact).astype(jnp.bfloat16)
    out_terms = jnp.einsum("tri,rkio->trko", hidden, w_out, preferred_element_type=jnp.float32)
    out_send = chip_sums(out_terms, out_flat)

    w_out_part = jnp.einsum("tri,rkto->rkio", hidden, grad_sel, preferred_element_type=jnp.float32)
    w_out_grad = dp_total(w_out_part)

    hid_grad = jnp.einsum("rkto,rkio->tri", grad_sel, w_out, preferred_element_type=jnp.float32)
    pre_grad = (hid_grad * gelu_slope(preact)).astype(jnp.bfloat16)
    in_terms = jnp.einsum("tro,rkio->trki", pre_grad, w_in, preferred_element_type=jnp.float32)
    in_send = chip_sums(in_terms, in_flat)
    got = lax.all_to_all(jnp.stack([out_send, in_send], axis=0), "chip", split_axis=2, concat_axis=2, tiled=True)
    outputs = finish(got[0])
    in_grad = finish(got[1])
    w_in_part = jnp.einsum("rkti,tro->rkio", in_sel, pre_grad, preferred_element_type=jnp.float32)
    w_in_grad = dp_total(w_in_part)
    return (outputs, in_grad, w_in_grad, w_out_grad)


def solution(mesh):
    n_dp, n_mp = mesh.shape["dp"], mesh.shape["mp"]
    pair = 2 if n_mp % 2 == 0 else 1
    split = Mesh(mesh.devices.reshape(n_dp, n_mp // pair, pair), ("dp", "chip", "core"))
    cols = ("chip", "core")
    return jax.shard_map(
        per_device,
        mesh=split,
        in_specs=(
            P("dp", cols),
            P("dp", cols),
            P(cols, None, None, None),
            P(cols, None),
            P(cols, None, None, None),
            P(cols, None),
        ),
        out_specs=(
            P("dp", cols),
            P("dp", cols),
            P(cols, None, None, None),
            P(cols, None, None, None),
        ),
        check_vma=False,
    )
```
